32 devices in a mesh: slab: 2 (over y), blk: 4 (over z), bag: 2 (over x), sub: 2 (over core).
Axes of the slice: x: 2, y: 2, z: 4, core: 2. Of those that a mesh axis runs over, the one named last changes fastest.
Arguments:
- real_points: bfloat16 [64, 8192], P(None, ('slab', 'blk')), parts along dimension 1, may hold values from -4 to 4
- synth_points: bfloat16 [64, 8192], P(None, ('slab', 'blk')), parts along dimension 1, may hold values from -4 to 4
- real_cluster: int32 [8192], P(('slab', 'blk')), parts along dimension 0, may hold values from 0 to 3
- synth_cluster: int32 [8192], P(('slab', 'blk')), parts along dimension 0, may hold values from 0 to 3
- real_weight: int32 [32, 8192], P('bag', ('slab', 'blk')), parts along dimension 1, may hold values from 0 to 4
- synth_weight: int32 [32, 8192], P('bag', ('slab', 'blk')), parts along dimension 1, may hold values from 0 to 4
- pair_block: int32 [64, 2], P(('slab', 'blk', 'sub')), parts along dimension 0, may hold values from 0 to 7, as said below
- pair_row: int32 [64, 2], P(('slab', 'blk', 'sub')), parts along dimension 0, may hold values from 0 to 7
- pair_count: int32 [64], P(('slab', 'blk', 'sub')), parts along dimension 0, may hold values from 1 to 2, as said below
Outputs:
- real_potential: float32 [32, 8192], P('bag', ('slab', 'blk')), parts along dimension 1
- synth_potential: float32 [32, 8192], P('bag', ('slab', 'blk')), parts along dimension 1
The draws below stay inside these ranges and needn't reach their ends.
There are 2 independent parts, one for each index of `slab`. The reference program is written for one: setup_inputs(seed, part) draws one part's arguments, and reference() takes and returns one part's arrays. A program takes and returns all parts, laid end to end along the dimension named above; each array names one. Nothing has to cross between parts.
Inputs may be any that keep to these rules, and one draw needn't show every extreme that they name: `pair_block`: row 4 * (2 * b + s) + p belongs to the device at blk index b and sub index s; all listed pairs of the whole list are distinct. `pair_count`: in every draw all devices of one sub index list 2 pairs with one blk index.
All inputs are finite; a program needn't handle non-finite values.
Results may differ from the reference program's by a relative error of at most 0.0015.
Values may be sent and summed in bfloat16 or wider, within the bound.
No kernel may reach another device: no remote copies, remote signals or barrier semaphores. Data moves between devices by JAX's collectives and lax.ppermute only.
A program may use at most 64 MiB of HBM per device.

```python
import math
import jax
import jax.numpy as jnp
from jax import lax

D = 64
BLOCK = 128
M = 32
XB = 8
PEER_CAP = 2
ITERS = 2
NPTS = 4096
N_BLK = 4
N_SUB = 2


def scaled_points(key, low_end, high_end):
    key_base, key_scale = jax.random.split(key, 2)
    base_draw = jax.random.truncated_normal(key_base, -4.0, 4.0, (D, NPTS), jnp.float32)
    point_scale = jnp.exp(jax.random.uniform(key_scale, (1, NPTS), jnp.float32, math.log(low_end), math.log(high_end)))
    values = base_draw * point_scale / math.sqrt(D)
    return jnp.clip(values, -4.0, 4.0).astype(jnp.bfloat16)


def draw_real_points(key, part):
    return scaled_points(jax.random.fold_in(key, 11), 0.6, 1.8)


def draw_synth_points(key, part):
    return scaled_points(jax.random.fold_in(key, 13), 0.6, 1.8)


def pair_lists(key):
    subkeys = jax.random.split(jax.random.fold_in(key, 29), 5)
    askers = N_BLK * N_SUB
    load_level = jax.random.randint(subkeys[0], (askers, 1), 1, PEER_CAP + 1)
    counts = 1 + jax.random.randint(subkeys[1], (askers, N_BLK), 0, 720720) % load_level
    hot_peer = jax.random.randint(subkeys[2], (), 0, N_BLK)
    hot_sub = jax.random.randint(subkeys[3], (), 0, N_SUB)
    asker_ids = jnp.arange(askers, dtype=jnp.int32)[:, None]
    peer_ids = jnp.arange(N_BLK, dtype=jnp.int32)[None, :]
    counts = jnp.where((asker_ids % N_SUB == hot_sub) & (peer_ids == hot_peer), PEER_CAP, counts)
    picked = jax.vmap(lambda one_key: jax.random.permutation(one_key, XB * XB)[:N_SUB * PEER_CAP])(jax.random.split(subkeys[4], N_BLK * N_BLK))
    picked = picked.reshape(N_BLK, N_BLK, PEER_CAP, N_SUB).transpose(0, 3, 1, 2).reshape(askers * N_BLK, PEER_CAP)
    return ((picked % XB).astype(jnp.int32), (picked // XB).astype(jnp.int32), counts.reshape(askers * N_BLK).astype(jnp.int32))


def draw_pair_block(key, part):
    return pair_lists(key)[0]


def draw_pair_row(key, part):
    return pair_lists(key)[1]


def draw_pair_count(key, part):
    return pair_lists(key)[2]


def place_ends(result, stream_key, smallest, high):
    dims = result.shape
    spot = [jax.random.randint(jax.random.fold_in(stream_key, axis), (), 0, dims[axis]) for axis in range(len(dims))]
    result = result.at[tuple(spot)].set(smallest)
    longest = dims.index(max(dims))
    spot[longest] = (spot[longest] + 1) % dims[longest]
    return result.at[tuple(spot)].set(high)


def setup_inputs(seed: int = 0, part: int = 0) -> dict:
    streams_of = jax.random.split(jax.random.key(seed), 10)
    own_keys = jax.random.split(jax.random.fold_in(streams_of[9], part), 10)
    real_points = draw_real_points(jax.random.fold_in(jax.random.fold_in(streams_of[9], part), 71), part)
    synth_points = draw_synth_points(jax.random.fold_in(jax.random.fold_in(streams_of[9], part), 71), part)
    real_cluster = place_ends(jax.random.randint(own_keys[2], (NPTS,), 0, 4), jax.random.fold_in(own_keys[2], 1), 0, 3).astype(jnp.int32)
    synth_cluster = place_ends(jax.random.randint(own_keys[3], (NPTS,), 0, 4), jax.random.fold_in(own_keys[3], 1), 0, 3).astype(jnp.int32)
    real_weight = place_ends(jax.random.randint(own_keys[4], (M, NPTS), 0, 5), jax.random.fold_in(own_keys[4], 1), 0, 4).astype(jnp.int32)
    synth_weight = place_ends(jax.random.randint(own_keys[5], (M, NPTS), 0, 5), jax.random.fold_in(own_keys[5], 1), 0, 4).astype(jnp.int32)
    pair_block = draw_pair_block(jax.random.fold_in(jax.random.fold_in(streams_of[9], part), 71), part)
    pair_row = draw_pair_row(jax.random.fold_in(jax.random.fold_in(streams_of[9], part), 71), part)
    pair_count = draw_pair_count(jax.random.fold_in(jax.random.fold_in(streams_of[9], part), 71), part)
    return dict(real_points=real_points, synth_points=synth_points, real_cluster=real_cluster, synth_cluster=synth_cluster, real_weight=real_weight, synth_weight=synth_weight, pair_block=pair_block, pair_row=pair_row, pair_count=pair_count)


SMOOTH = 0.1
PENALTY = 0.3
SENTINEL = -1.0e30


def finish(log_weight, block_top, summed):
    spread = jnp.where(summed > 0.5, block_top + jnp.log(jnp.maximum(summed, 0.5)), 0.0)
    return SMOOTH * log_weight - SMOOTH * spread


def reference(real_points, synth_points, real_cluster, synth_cluster, real_weight, synth_weight, pair_block, pair_row, pair_count):
    total_blocks = XB * N_BLK
    listings = N_BLK * N_SUB * N_BLK
    listing = jnp.arange(listings, dtype=jnp.int32)
    asking = listing // N_BLK // N_SUB
    owners = listing % N_BLK
    usable = (jnp.arange(PEER_CAP, dtype=jnp.int32)[None, :] < pair_count[:, None]).reshape(-1)
    row_ids = (asking[:, None] * XB + pair_row).reshape(-1).astype(jnp.int32)
    col_ids = (owners[:, None] * XB + pair_block).reshape(-1).astype(jnp.int32)
    row_seg = jnp.where(usable, row_ids, total_blocks).astype(jnp.int32)
    col_seg = jnp.where(usable, col_ids, total_blocks).astype(jnp.int32)
    real_three = real_points.reshape(D, total_blocks, BLOCK)
    synth_three = synth_points.reshape(D, total_blocks, BLOCK)
    real_tags = real_cluster.reshape(total_blocks, BLOCK)
    synth_tags = synth_cluster.reshape(total_blocks, BLOCK)
    log_real = jnp.log(real_weight.astype(jnp.float32) + 0.5).reshape(M, total_blocks, BLOCK)
    log_synth = jnp.log(synth_weight.astype(jnp.float32) + 0.5).reshape(M, total_blocks, BLOCK)

    def block_cost(row_id, col_id):
        real_block = lax.dynamic_index_in_dim(real_three, row_id, 1, keepdims=False)
        synth_block = lax.dynamic_index_in_dim(synth_three, col_id, 1, keepdims=False)
        inner_prod = jnp.dot(real_block.T, synth_block, preferred_element_type=jnp.float32)
        real_sq = jnp.sum(jnp.square(real_block.astype(jnp.float32)), axis=0)
        synth_sq = jnp.sum(jnp.square(synth_block.astype(jnp.float32)), axis=0)
        real_tag = lax.dynamic_index_in_dim(real_tags, row_id, 0, keepdims=False)
        synth_tag = lax.dynamic_index_in_dim(synth_tags, col_id, 0, keepdims=False)
        differ = (real_tag[:, None] != synth_tag[None, :]).astype(jnp.float32)
        return 0.5 * real_sq[:, None] + 0.5 * synth_sq[None, :] - inner_prod + PENALTY * differ

    def fold_all(highest, mass_sum, segment):
        block_top = jnp.full((total_blocks + 1, M, BLOCK), SENTINEL, jnp.float32).at[segment].max(highest)
        scaled = mass_sum * jnp.exp(highest - block_top[segment])
        summed = jnp.zeros((total_blocks + 1, M, BLOCK), jnp.float32).at[segment].add(scaled)
        return jnp.transpose(block_top[:total_blocks], (1, 0, 2)), jnp.transpose(summed[:total_blocks], (1, 0, 2))

    synth_pot = jnp.zeros((M, total_blocks, BLOCK), jnp.float32)
    real_pot = jnp.zeros((M, total_blocks, BLOCK), jnp.float32)
    for sweep_index in range(ITERS):
        def row_part(pair_ids, synth_now=synth_pot):
            pair_cost = block_cost(pair_ids[0], pair_ids[1])
            panel_rows = lax.dynamic_index_in_dim(synth_now, pair_ids[1], 1, keepdims=False)
            scores = (panel_rows[:, None, :] - pair_cost[None]) / SMOOTH
            highest = jnp.max(scores, axis=2)
            return highest, jnp.sum(jnp.exp(scores - highest[:, :, None]), axis=2)

        highest, mass_sum = lax.map(row_part, (row_ids, col_ids))
        block_top, summed = fold_all(highest, mass_sum, row_seg)
        real_pot = finish(log_real, block_top, summed)

        def col_part(pair_ids, real_now=real_pot):
            pair_cost = block_cost(pair_ids[0], pair_ids[1])
            panel_rows = lax.dynamic_index_in_dim(real_now, pair_ids[0], 1, keepdims=False)
            scores = (panel_rows[:, :, None] - pair_cost[None]) / SMOOTH
            highest = jnp.max(scores, axis=1)
            return highest, jnp.sum(jnp.exp(scores - highest[:, None, :]), axis=1)

        highest, mass_sum = lax.map(col_part, (row_ids, col_ids))
        block_top, summed = fold_all(highest, mass_sum, col_seg)
        synth_pot = finish(log_synth, block_top, summed)
    return real_pot.reshape(M, total_blocks * BLOCK), synth_pot.reshape(M, total_blocks * BLOCK)
```

```python
import jax
import jax.numpy as jnp
from jax import lax
from jax.sharding import PartitionSpec as P

BLOCK = 128
ITERS = 2


SMOOTH = 0.1
PENALTY = 0.3
SENTINEL = -1e30


def join_parts(earlier, latter):
    larger = jnp.maximum(earlier[0], latter[0])
    return (
        larger,
        earlier[1] * jnp.exp(earlier[0] - larger) + latter[1] * jnp.exp(latter[0] - larger),
    )


def fold_blocks(highest, mass_sum, owners, blocks):
    matches = owners[:, None] == jnp.arange(blocks, dtype=jnp.int32)[None, :]
    match_mask = matches[None, :, :, None]
    block_top = jnp.max(jnp.where(match_mask, highest[:, :, None, :], SENTINEL), axis=1)
    slot_top = jnp.take(block_top, owners, axis=1)
    scaled = mass_sum * jnp.exp(highest - slot_top)
    summed = jnp.sum(jnp.where(match_mask, scaled[:, :, None, :], 0.0), axis=1)
    return (block_top, summed)


def finish(log_weight, block_top, summed):
    spread = jnp.where(summed > 0.5, block_top + jnp.log(jnp.maximum(summed, 0.5)), 0.0)
    return SMOOTH * log_weight - SMOOTH * spread


def slot_costs(slot_real, slot_real_tag, slot_synth, slot_synth_tag):
    inner_prod = jnp.einsum(
        "dgi,dgj->gij", slot_real, slot_synth, preferred_element_type=jnp.float32
    )
    real_sq = jnp.sum(jnp.square(slot_real.astype(jnp.float32)), axis=0)
    synth_sq = jnp.sum(jnp.square(slot_synth.astype(jnp.float32)), axis=0)
    differ = (slot_real_tag[:, :, None] != slot_synth_tag[:, None, :]).astype(jnp.float32)
    return 0.5 * real_sq[:, :, None] + 0.5 * synth_sq[:, None, :] - inner_prod + PENALTY * differ


def lse_parts(scores, axis):
    highest = jnp.max(scores, axis=axis)
    mass_sum = jnp.sum(jnp.exp(scores - jnp.expand_dims(highest, axis)), axis=axis)
    return (highest, mass_sum)


def make_shards(n_sub):
    group = ("blk", "sub")

    def sub_join(parts):
        if n_sub == 2:
            other = lax.ppermute(jnp.stack(parts), "sub", [(0, 1), (1, 0)])
            return join_parts(parts, (other[0], other[1]))
        pieces = lax.all_gather(jnp.stack(parts), "sub")
        subtotal = (pieces[0, 0], pieces[0, 1])
        for index in range(1, n_sub):
            subtotal = join_parts(subtotal, (pieces[index, 0], pieces[index, 1]))
        return subtotal

    def shards(
        real_points,
        synth_points,
        real_cluster,
        synth_cluster,
        real_weight,
        synth_weight,
        pair_block,
        pair_row,
        pair_count,
    ):
        features, point_count = real_points.shape
        blocks = point_count // BLOCK
        marginals = real_weight.shape[0]
        peer_count, capacity = pair_block.shape
        slot_count = peer_count * capacity
        my_sub = lax.axis_index("sub")
        own_real = real_points.reshape(features, blocks, BLOCK)
        real_tags = real_cluster.reshape(blocks, BLOCK)
        own_synth = jnp.concatenate(
            [synth_points, synth_cluster.astype(jnp.bfloat16)[None, :]], axis=0
        ).reshape(features + 1, blocks, BLOCK)
        log_real = jnp.log(real_weight.astype(jnp.float32) + 0.5).reshape(marginals, blocks, BLOCK)
        log_synth = jnp.log(synth_weight.astype(jnp.float32) + 0.5).reshape(marginals, blocks, BLOCK)
        listed = lax.broadcasted_iota(jnp.int32, (peer_count, capacity), 1) < pair_count[:, None]
        wanted = jnp.where(listed, pair_block, 0)
        rows_used = jnp.where(listed, pair_row, 0).reshape(slot_count)
        usable = listed.reshape(slot_count)[None, :, None]

        asked = jnp.broadcast_to(wanted[:, None, :], (peer_count, n_sub, capacity))
        requested = lax.all_to_all(
            asked.reshape(peer_count * n_sub, capacity), group, split_axis=0, concat_axis=0, tiled=True
        )
        requested_all = requested.reshape(peer_count * n_sub * capacity)
        requested_same = lax.dynamic_index_in_dim(
            requested.reshape(peer_count, n_sub, capacity), my_sub, axis=1, keepdims=False
        ).reshape(slot_count)

        far = lax.all_to_all(
            jnp.take(own_synth, requested_same, axis=1).reshape(features + 1, peer_count, capacity, BLOCK),
            "blk",
            split_axis=1,
            concat_axis=1,
            tiled=True,
        ).reshape(features + 1, slot_count, BLOCK)
        far_y = far[:features]
        far_tags = far[features]
        slot_x = jnp.take(own_real, rows_used, axis=1)
        slot_tags = jnp.take(real_tags, rows_used, axis=0).astype(jnp.bfloat16)
        cost = slot_costs(slot_x, slot_tags, far_y, far_tags)

        synth_pot = jnp.zeros((marginals, blocks, BLOCK), jnp.float32)
        real_pot = jnp.zeros((marginals, blocks, BLOCK), jnp.float32)
        for sweep_index in range(ITERS):
            if sweep_index == 0:
                panel = jnp.zeros((marginals, slot_count, BLOCK), jnp.float32)
            else:
                panel = lax.all_to_all(
                    jnp.take(synth_pot, requested_same, axis=1).reshape(
                        marginals, peer_count, capacity, BLOCK
                    ),
                    "blk",
                    split_axis=1,
                    concat_axis=1,
                    tiled=True,
                ).reshape(marginals, slot_count, BLOCK)
            scores = (panel[:, :, None, :] - cost[None]) / SMOOTH
            highest, mass_sum = lse_parts(scores, 3)
            highest = jnp.where(usable, highest, SENTINEL)
            mass_sum = jnp.where(usable, mass_sum, 0.0)
            block_top, summed = fold_blocks(highest, mass_sum, rows_used, blocks)
            block_top, summed = sub_join((block_top, summed))
            real_pot = finish(log_real, block_top, summed)

            own_rows = jnp.take(real_pot, rows_used, axis=1)
            scores = (own_rows[:, :, :, None] - cost[None]) / SMOOTH
            highest, mass_sum = lse_parts(scores, 2)
            highest = jnp.where(usable, highest, SENTINEL)
            mass_sum = jnp.where(usable, mass_sum, 0.0)
            outgoing = jnp.stack([highest, mass_sum]).reshape(2, marginals, peer_count, 1, capacity, BLOCK)
            outgoing = jnp.broadcast_to(
                outgoing, (2, marginals, peer_count, n_sub, capacity, BLOCK)
            ).reshape(2, marginals, peer_count * n_sub * capacity, BLOCK)
            back = lax.all_to_all(outgoing, group, split_axis=2, concat_axis=2, tiled=True)
            block_top, summed = fold_blocks(back[0], back[1], requested_all, blocks)
            synth_pot = finish(log_synth, block_top, summed)
        return (real_pot.reshape(marginals, point_count), synth_pot.reshape(marginals, point_count))

    return shards


def solution(mesh):
    placed = (
        P(None, ("slab", "blk")),
        P(None, ("slab", "blk")),
        P(("slab", "blk")),
        P(("slab", "blk")),
        P("bag", ("slab", "blk")),
        P("bag", ("slab", "blk")),
        P(("slab", "blk", "sub"), None),
        P(("slab", "blk", "sub"), None),
        P(("slab", "blk", "sub")),
    )
    return jax.shard_map(
        make_shards(mesh.shape["sub"]),
        mesh=mesh,
        in_specs=placed,
        out_specs=(P("bag", ("slab", "blk")), P("bag", ("slab", "blk"))),
        check_vma=False,
    )
```

```python
import jax
import jax.numpy as jnp
from jax import lax
from jax.sharding import PartitionSpec as P

BLOCK = 128
ITERS = 2


SMOOTH = 0.1
PENALTY = 0.3
SENTINEL = -1e30


def join_parts(earlier, latter):
    larger = jnp.maximum(earlier[0], latter[0])
    return (
        larger,
        earlier[1] * jnp.exp(earlier[0] - larger) + latter[1] * jnp.exp(latter[0] - larger),
    )


def pick(values, ids, blocks):
    hits = ids[:, None] == jnp.arange(blocks, dtype=jnp.int32)[None, :]
    chosen = jnp.where(hits[None, :, :, None], values[:, None, :, :], jnp.zeros((), values.dtype))
    return jnp.sum(chosen, axis=2, dtype=values.dtype)


def fold_blocks(highest, mass_sum, owners, blocks):
    matches = owners[:, None] == jnp.arange(blocks, dtype=jnp.int32)[None, :]
    match_mask = matches[None, :, :, None]
    block_top = jnp.max(jnp.where(match_mask, highest[:, :, None, :], SENTINEL), axis=1)
    slot_top = pick(block_top, owners, blocks)
    scaled = mass_sum * jnp.exp(highest - slot_top)
    summed = jnp.sum(jnp.where(match_mask, scaled[:, :, None, :], 0.0), axis=1)
    return (block_top, summed)


def fold_lse(lse, owners, blocks):
    matches = owners[:, None] == jnp.arange(blocks, dtype=jnp.int32)[None, :]
    match_mask = matches[None, :, :, None]
    block_top = jnp.max(jnp.where(match_mask, lse[:, :, None, :], SENTINEL), axis=1)
    slot_top = pick(block_top, owners, blocks)
    scaled = jnp.where(lse > 0.5 * SENTINEL, jnp.exp(lse - slot_top), 0.0)
    summed = jnp.sum(jnp.where(match_mask, scaled[:, :, None, :], 0.0), axis=1)
    return (block_top, summed)


def finish(log_weight, block_top, summed):
    spread = jnp.where(summed > 0.5, block_top + jnp.log(jnp.maximum(summed, 0.5)), 0.0)
    return SMOOTH * log_weight - SMOOTH * spread


def slot_costs(slot_real, slot_real_tag, slot_synth, slot_synth_tag):
    inner_prod = jnp.einsum(
        "dgi,dgj->gij", slot_real, slot_synth, preferred_element_type=jnp.float32
    )
    real_sq = jnp.sum(jnp.square(slot_real.astype(jnp.float32)), axis=0)
    synth_sq = jnp.sum(jnp.square(slot_synth.astype(jnp.float32)), axis=0)
    differ = (slot_real_tag[:, :, None] != slot_synth_tag[:, None, :]).astype(jnp.float32)
    return 0.5 * real_sq[:, :, None] + 0.5 * synth_sq[:, None, :] - inner_prod + PENALTY * differ


def lse_parts(scores, axis):
    highest = jnp.max(scores, axis=axis)
    mass_sum = jnp.sum(jnp.exp(scores - jnp.expand_dims(highest, axis)), axis=axis)
    return (highest, mass_sum)


def make_shards(n_sub):
    group = ("blk", "sub")

    def sub_join(parts):
        if n_sub == 2:
            other = lax.ppermute(jnp.stack(parts), "sub", [(0, 1), (1, 0)])
            return join_parts(parts, (other[0], other[1]))
        pieces = lax.all_gather(jnp.stack(parts), "sub")
        subtotal = (pieces[0, 0], pieces[0, 1])
        for index in range(1, n_sub):
            subtotal = join_parts(subtotal, (pieces[index, 0], pieces[index, 1]))
        return subtotal

    def shards(
        real_points,
        synth_points,
        real_cluster,
        synth_cluster,
        real_weight,
        synth_weight,
        pair_block,
        pair_row,
        pair_count,
    ):
        features, point_count = real_points.shape
        blocks = point_count // BLOCK
        marginals = real_weight.shape[0]
        peer_count, capacity = pair_block.shape
        slot_count = peer_count * capacity
        my_sub = lax.axis_index("sub")
        own_real = real_points.reshape(features, blocks, BLOCK)
        real_tags = real_cluster.reshape(blocks, BLOCK)
        own_synth = jnp.concatenate(
            [synth_points, synth_cluster.astype(jnp.bfloat16)[None, :]], axis=0
        ).reshape(features + 1, blocks, BLOCK)
        log_real = jnp.log(real_weight.astype(jnp.float32) + 0.5).reshape(marginals, blocks, BLOCK)
        log_synth = jnp.log(synth_weight.astype(jnp.float32) + 0.5).reshape(marginals, blocks, BLOCK)
        listed = lax.broadcasted_iota(jnp.int32, (peer_count, capacity), 1) < pair_count[:, None]
        wanted = jnp.where(listed, pair_block, 0)
        rows_used = jnp.where(listed, pair_row, 0).reshape(slot_count)
        usable = listed.reshape(slot_count)[None, :, None]

        asked = jnp.broadcast_to(wanted[:, None, :], (peer_count, n_sub, capacity))
        requested = lax.all_to_all(
            asked.reshape(peer_count * n_sub, capacity), group, split_axis=0, concat_axis=0, tiled=True
        )
        requested_all = requested.reshape(peer_count * n_sub * capacity)
        requested_same = lax.dynamic_index_in_dim(
            requested.reshape(peer_count, n_sub, capacity), my_sub, axis=1, keepdims=False
        ).reshape(slot_count)

        far = lax.all_to_all(
            pick(own_synth, requested_same, blocks).reshape(features + 1, peer_count, capacity, BLOCK),
            "blk",
            split_axis=1,
            concat_axis=1,
            tiled=True,
        ).reshape(features + 1, slot_count, BLOCK)
        far_y = far[:features]
        far_tags = far[features]
        slot_x = pick(own_real, rows_used, blocks)
        slot_tags = pick(real_tags[None], rows_used, blocks)[0].astype(jnp.bfloat16)
        cost = slot_costs(slot_x, slot_tags, far_y, far_tags)
        cost_cols = cost / SMOOTH
        cost_rows = jnp.transpose(cost_cols, (0, 2, 1))

        synth_pot = jnp.zeros((marginals, blocks, BLOCK), jnp.float32)
        real_pot = jnp.zeros((marginals, blocks, BLOCK), jnp.float32)
        for sweep_index in range(ITERS):
            if sweep_index == 0:
                panel = jnp.zeros((marginals, slot_count, BLOCK), jnp.float32)
            else:
                panel = lax.all_to_all(
                    pick(synth_pot, requested_same, blocks).reshape(
                        marginals, peer_count, capacity, BLOCK
                    ),
                    "blk",
                    split_axis=1,
                    concat_axis=1,
                    tiled=True,
                ).reshape(marginals, slot_count, BLOCK)
            scores = (panel / SMOOTH)[:, :, :, None] - cost_rows[None]
            highest, mass_sum = lse_parts(scores, 2)
            highest = jnp.where(usable, highest, SENTINEL)
            mass_sum = jnp.where(usable, mass_sum, 0.0)
            block_top, summed = fold_blocks(highest, mass_sum, rows_used, blocks)
            block_top, summed = sub_join((block_top, summed))
            real_pot = finish(log_real, block_top, summed)

            own_rows = pick(real_pot, rows_used, blocks)
            scores = (own_rows / SMOOTH)[:, :, :, None] - cost_cols[None]
            highest, mass_sum = lse_parts(scores, 2)
            lse = jnp.where(usable, highest + jnp.log(mass_sum), SENTINEL)
            outgoing = lse.reshape(marginals, peer_count, 1, capacity, BLOCK)
            outgoing = jnp.broadcast_to(
                outgoing, (marginals, peer_count, n_sub, capacity, BLOCK)
            ).reshape(marginals, peer_count * n_sub * capacity, BLOCK)
            back = lax.all_to_all(outgoing, group, split_axis=1, concat_axis=1, tiled=True)
            block_top, summed = fold_lse(back, requested_all, blocks)
            synth_pot = finish(log_synth, block_top, summed)
        return (real_pot.reshape(marginals, point_count), synth_pot.reshape(marginals, point_count))

    return shards


def solution(mesh):
    placed = (
        P(None, ("slab", "blk")),
        P(None, ("slab", "blk")),
        P(("slab", "blk")),
        P(("slab", "blk")),
        P("bag", ("slab", "blk")),
        P("bag", ("slab", "blk")),
        P(("slab", "blk", "sub"), None),
        P(("slab", "blk", "sub"), None),
        P(("slab", "blk", "sub")),
    )
    return jax.shard_map(
        make_shards(mesh.shape["sub"]),
        mesh=mesh,
        in_specs=placed,
        out_specs=(P("bag", ("slab", "blk")), P("bag", ("slab", "blk"))),
        check_vma=False,
    )
```

```python
import jax
import jax.numpy as jnp
from jax import lax
from jax.sharding import PartitionSpec as P

BLOCK = 128
ITERS = 2


SMOOTH = 0.1
PENALTY = 0.3
SENTINEL = -1e30


def join_parts(earlier, latter):
    larger = jnp.maximum(earlier[0], latter[0])
    return (
        larger,
        earlier[1] * jnp.exp(earlier[0] - larger) + latter[1] * jnp.exp(latter[0] - larger),
    )


def pick_rows(values, ids, blocks):
    hits = ids[:, None] == jnp.arange(blocks, dtype=jnp.int32)[None, :]
    chosen = jnp.where(hits[:, None, :, None], values[None], jnp.zeros((), values.dtype))
    return jnp.sum(chosen, axis=2, dtype=values.dtype)


def pick_lead(values, ids):
    hits = ids[:, None] == jnp.arange(values.shape[0], dtype=jnp.int32)[None, :]
    hits = hits.reshape(hits.shape + (1,) * (values.ndim - 1))
    return jnp.sum(jnp.where(hits, values[None], jnp.zeros((), values.dtype)), axis=1, dtype=values.dtype)


def fold_blocks(highest, mass_sum, owners, blocks):
    matches = owners[:, None] == jnp.arange(blocks, dtype=jnp.int32)[None, :]
    match_mask = matches[:, None, :, None]
    block_top = jnp.max(jnp.where(match_mask, highest[:, :, None, :], SENTINEL), axis=0)
    slot_top = pick_rows(block_top, owners, blocks)
    scaled = mass_sum * jnp.exp(highest - slot_top)
    summed = jnp.sum(jnp.where(match_mask, scaled[:, :, None, :], 0.0), axis=0)
    return (block_top, summed)


def fold_lse(lse, owners, blocks):
    matches = owners[:, None] == jnp.arange(blocks, dtype=jnp.int32)[None, :]
    match_mask = matches[:, None, :, None]
    block_top = jnp.max(jnp.where(match_mask, lse[:, :, None, :], SENTINEL), axis=0)
    slot_top = pick_rows(block_top, owners, blocks)
    scaled = jnp.where(lse > 0.5 * SENTINEL, jnp.exp(lse - slot_top), 0.0)
    summed = jnp.sum(jnp.where(match_mask, scaled[:, :, None, :], 0.0), axis=0)
    return (block_top, summed)


def finish(log_weight, block_top, summed):
    spread = jnp.where(summed > 0.5, block_top + jnp.log(jnp.maximum(summed, 0.5)), 0.0)
    return SMOOTH * log_weight - SMOOTH * spread


def slot_costs(slot_real, slot_real_tag, slot_synth, slot_synth_tag):
    inner_prod = jnp.einsum(
        "gdi,gdj->gij", slot_real, slot_synth, preferred_element_type=jnp.float32
    )
    real_sq = jnp.sum(jnp.square(slot_real.astype(jnp.float32)), axis=1)
    synth_sq = jnp.sum(jnp.square(slot_synth.astype(jnp.float32)), axis=1)
    differ = (slot_real_tag[:, :, None] != slot_synth_tag[:, None, :]).astype(jnp.float32)
    return 0.5 * real_sq[:, :, None] + 0.5 * synth_sq[:, None, :] - inner_prod + PENALTY * differ


def lse_parts(scores, axis):
    highest = jnp.max(scores, axis=axis)
    mass_sum = jnp.sum(jnp.exp(scores - jnp.expand_dims(highest, axis)), axis=axis)
    return (highest, mass_sum)


def make_shards(n_blk, n_sub):
    def sub_join(parts):
        if n_sub == 2:
            other = lax.ppermute(jnp.stack(parts), "sub", [(0, 1), (1, 0)])
            return join_parts(parts, (other[0], other[1]))
        pieces = lax.all_gather(jnp.stack(parts), "sub")
        subtotal = (pieces[0, 0], pieces[0, 1])
        for index in range(1, n_sub):
            subtotal = join_parts(subtotal, (pieces[index, 0], pieces[index, 1]))
        return subtotal

    def send_up(chunks):
        moved = [chunks[0]]
        for offset in range(1, n_blk):
            perm = [(index, (index + offset) % n_blk) for index in range(n_blk)]
            moved.append(lax.ppermute(chunks[offset], "blk", perm))
        return moved

    def send_down(chunks):
        moved = [chunks[0]]
        for offset in range(1, n_blk):
            perm = [(index, (index - offset) % n_blk) for index in range(n_blk)]
            moved.append(lax.ppermute(chunks[offset], "blk", perm))
        return moved

    def shards(
        real_points,
        synth_points,
        real_cluster,
        synth_cluster,
        real_weight,
        synth_weight,
        pair_block,
        pair_row,
        pair_count,
    ):
        features, point_count = real_points.shape
        blocks = point_count // BLOCK
        marginals = real_weight.shape[0]
        peer_count, capacity = pair_block.shape
        slot_count = peer_count * capacity
        my_blk = lax.axis_index("blk")
        own_real = real_points.reshape(features, blocks, BLOCK)
        real_tags = real_cluster.reshape(1, blocks, BLOCK).astype(jnp.bfloat16)
        own_synth = jnp.concatenate(
            [synth_points, synth_cluster.astype(jnp.bfloat16)[None, :]], axis=0
        ).reshape(features + 1, blocks, BLOCK)
        log_real = jnp.log(real_weight.astype(jnp.float32) + 0.5).reshape(marginals, blocks, BLOCK)
        log_synth = jnp.log(synth_weight.astype(jnp.float32) + 0.5).reshape(marginals, blocks, BLOCK)

        peers = (my_blk + jnp.arange(peer_count, dtype=jnp.int32)) % peer_count
        listed = lax.broadcasted_iota(jnp.int32, (peer_count, capacity), 1) < pair_count[:, None]
        wanted = pick_lead(jnp.where(listed, pair_block, 0), peers)
        rows_used = pick_lead(jnp.where(listed, pair_row, 0), peers).reshape(slot_count)
        usable = pick_lead(listed.astype(jnp.int32), peers).reshape(slot_count)[:, None, None] > 0

        requested = jnp.stack(send_up([wanted[offset] for offset in range(peer_count)]))
        far = jnp.concatenate(
            send_down([pick_rows(own_synth, requested[offset], blocks) for offset in range(peer_count)]),
            axis=0,
        )
        requested = requested.reshape(slot_count)
        far_y = far[:, :features]
        far_tags = far[:, features]
        slot_x = pick_rows(own_real, rows_used, blocks)
        slot_tags = pick_rows(real_tags, rows_used, blocks)[:, 0]
        cost = slot_costs(slot_x, slot_tags, far_y, far_tags)
        cost_cols = cost / SMOOTH
        cost_rows = jnp.transpose(cost_cols, (0, 2, 1))

        synth_pot = jnp.zeros((marginals, blocks, BLOCK), jnp.float32)
        real_pot = jnp.zeros((marginals, blocks, BLOCK), jnp.float32)
        for sweep_index in range(ITERS):
            if sweep_index == 0:
                panel = jnp.zeros((slot_count, marginals, BLOCK), jnp.float32)
            else:
                panel = jnp.concatenate(
                    send_down(
                        [
                            pick_rows(synth_pot, requested[offset * capacity : (offset + 1) * capacity], blocks)
                            for offset in range(peer_count)
                        ]
                    ),
                    axis=0,
                )
            scores = (panel / SMOOTH)[:, :, :, None] - cost_rows[:, None]
            highest, mass_sum = lse_parts(scores, 2)
            highest = jnp.where(usable, highest, SENTINEL)
            mass_sum = jnp.where(usable, mass_sum, 0.0)
            block_top, summed = fold_blocks(highest, mass_sum, rows_used, blocks)
            block_top, summed = sub_join((block_top, summed))
            real_pot = finish(log_real, block_top, summed)

            own_rows = pick_rows(real_pot, rows_used, blocks)
            scores = (own_rows / SMOOTH)[:, :, :, None] - cost_cols[:, None]
            highest, mass_sum = lse_parts(scores, 2)
            lse = jnp.where(usable, highest + jnp.log(mass_sum), SENTINEL)
            back = jnp.concatenate(
                send_up([lse[offset * capacity : (offset + 1) * capacity] for offset in range(peer_count)]),
                axis=0,
            )
            block_top, summed = fold_lse(back, requested, blocks)
            block_top, summed = sub_join((block_top, summed))
            synth_pot = finish(log_synth, block_top, summed)
        return (real_pot.reshape(marginals, point_count), synth_pot.reshape(marginals, point_count))

    return shards


def solution(mesh):
    placed = (
        P(None, ("slab", "blk")),
        P(None, ("slab", "blk")),
        P(("slab", "blk")),
        P(("slab", "blk")),
        P("bag", ("slab", "blk")),
        P("bag", ("slab", "blk")),
        P(("slab", "blk", "sub"), None),
        P(("slab", "blk", "sub"), None),
        P(("slab", "blk", "sub")),
    )
    return jax.shard_map(
        make_shards(mesh.shape["blk"], mesh.shape["sub"]),
        mesh=mesh,
        in_specs=placed,
        out_specs=(P("bag", ("slab", "blk")), P("bag", ("slab", "blk"))),
        check_vma=False,
    )
```

```python
import jax
import jax.numpy as jnp
from jax import lax
from jax.experimental import pallas as pl
from jax.experimental.pallas import tpu as pltpu
from jax.sharding import PartitionSpec as P

BLOCK = 128
ITERS = 2


SMOOTH = 0.1
PENALTY = 0.3
SENTINEL = -1e30


def join_parts(earlier, latter):
    larger = jnp.maximum(earlier[0], latter[0])
    return (
        larger,
        earlier[1] * jnp.exp(earlier[0] - larger) + latter[1] * jnp.exp(latter[0] - larger),
    )


def pick_rows(values, ids, blocks):
    hits = ids[:, None] == jnp.arange(blocks, dtype=jnp.int32)[None, :]
    chosen = jnp.where(hits[:, None, :, None], values[None], jnp.zeros((), values.dtype))
    return jnp.sum(chosen, axis=2, dtype=values.dtype)


def pick_lead(values, ids):
    hits = ids[:, None] == jnp.arange(values.shape[0], dtype=jnp.int32)[None, :]
    hits = hits.reshape(hits.shape + (1,) * (values.ndim - 1))
    return jnp.sum(jnp.where(hits, values[None], jnp.zeros((), values.dtype)), axis=1, dtype=values.dtype)


def fold_blocks(highest, mass_sum, owners, blocks):
    matches = owners[:, None] == jnp.arange(blocks, dtype=jnp.int32)[None, :]
    match_mask = matches[:, None, :, None]
    block_top = jnp.max(jnp.where(match_mask, highest[:, :, None, :], SENTINEL), axis=0)
    slot_top = pick_rows(block_top, owners, blocks)
    scaled = mass_sum * jnp.exp(highest - slot_top)
    summed = jnp.sum(jnp.where(match_mask, scaled[:, :, None, :], 0.0), axis=0)
    return (block_top, summed)


def fold_lse(lse, owners, blocks):
    matches = owners[:, None] == jnp.arange(blocks, dtype=jnp.int32)[None, :]
    match_mask = matches[:, None, :, None]
    block_top = jnp.max(jnp.where(match_mask, lse[:, :, None, :], SENTINEL), axis=0)
    slot_top = pick_rows(block_top, owners, blocks)
    scaled = jnp.where(lse > 0.5 * SENTINEL, jnp.exp(lse - slot_top), 0.0)
    summed = jnp.sum(jnp.where(match_mask, scaled[:, :, None, :], 0.0), axis=0)
    return (block_top, summed)


def finish(log_weight, block_top, summed):
    spread = jnp.where(summed > 0.5, block_top + jnp.log(jnp.maximum(summed, 0.5)), 0.0)
    return SMOOTH * log_weight - SMOOTH * spread


def slot_costs(slot_real, slot_real_tag, slot_synth, slot_synth_tag):
    inner_prod = jnp.einsum(
        "gdi,gdj->gij", slot_real, slot_synth, preferred_element_type=jnp.float32
    )
    real_sq = jnp.sum(jnp.square(slot_real.astype(jnp.float32)), axis=1)
    synth_sq = jnp.sum(jnp.square(slot_synth.astype(jnp.float32)), axis=1)
    differ = (slot_real_tag[:, :, None] != slot_synth_tag[:, None, :]).astype(jnp.float32)
    return 0.5 * real_sq[:, :, None] + 0.5 * synth_sq[:, None, :] - inner_prod + PENALTY * differ


def lse_kernel(cost_ref, pot_ref, out_ref):
    slots, _, marginals = pot_ref.shape

    def one_slot(slot, carry):
        tile = cost_ref[slot]
        pots = pot_ref[slot]
        for marginal in range(marginals):
            scores = pots[:, marginal : marginal + 1] - tile
            highest = jnp.max(scores, axis=0, keepdims=True)
            mass_sum = jnp.sum(jnp.exp(scores - highest), axis=0, keepdims=True)
            out_ref[slot, pl.ds(marginal, 1), :] = highest + jnp.log(mass_sum)
        return carry

    lax.fori_loop(0, slots, one_slot, 0)


def slot_lse(cost, pots):
    slots, width, _ = cost.shape
    marginals = pots.shape[1]
    return pl.pallas_call(
        lse_kernel,
        out_shape=jax.ShapeDtypeStruct((slots, marginals, width), jnp.float32),
        in_specs=[pl.BlockSpec(memory_space=pltpu.VMEM)] * 2,
        out_specs=pl.BlockSpec(memory_space=pltpu.VMEM),
        cost_estimate=pl.CostEstimate(
            flops=6 * slots * marginals * width * width,
            transcendentals=slots * marginals * width * width,
            bytes_accessed=4 * (slots * width * width + 2 * slots * marginals * width),
        ),
    )(cost, jnp.transpose(pots, (0, 2, 1)))


def make_shards(n_blk, n_sub):
    def sub_join(parts):
        if n_sub == 2:
            other = lax.ppermute(jnp.stack(parts), "sub", [(0, 1), (1, 0)])
            return join_parts(parts, (other[0], other[1]))
        pieces = lax.all_gather(jnp.stack(parts), "sub")
        subtotal = (pieces[0, 0], pieces[0, 1])
        for index in range(1, n_sub):
            subtotal = join_parts(subtotal, (pieces[index, 0], pieces[index, 1]))
        return subtotal

    def send_up(chunks):
        moved = [chunks[0]]
        for offset in range(1, n_blk):
            perm = [(index, (index + offset) % n_blk) for index in range(n_blk)]
            moved.append(lax.ppermute(chunks[offset], "blk", perm))
        return moved

    def send_down(chunks):
        moved = [chunks[0]]
        for offset in range(1, n_blk):
            perm = [(index, (index - offset) % n_blk) for index in range(n_blk)]
            moved.append(lax.ppermute(chunks[offset], "blk", perm))
        return moved

    def shards(
        real_points,
        synth_points,
        real_cluster,
        synth_cluster,
        real_weight,
        synth_weight,
        pair_block,
        pair_row,
        pair_count,
    ):
        features, point_count = real_points.shape
        blocks = point_count // BLOCK
        marginals = real_weight.shape[0]
        peer_count, capacity = pair_block.shape
        slot_count = peer_count * capacity
        my_blk = lax.axis_index("blk")
        own_real = real_points.reshape(features, blocks, BLOCK)
        real_tags = real_cluster.reshape(1, blocks, BLOCK).astype(jnp.bfloat16)
        own_synth = jnp.concatenate(
            [synth_points, synth_cluster.astype(jnp.bfloat16)[None, :]], axis=0
        ).reshape(features + 1, blocks, BLOCK)
        log_real = jnp.log(real_weight.astype(jnp.float32) + 0.5).reshape(marginals, blocks, BLOCK)
        log_synth = jnp.log(synth_weight.astype(jnp.float32) + 0.5).reshape(marginals, blocks, BLOCK)

        peers = (my_blk + jnp.arange(peer_count, dtype=jnp.int32)) % peer_count
        listed = lax.broadcasted_iota(jnp.int32, (peer_count, capacity), 1) < pair_count[:, None]
        wanted = pick_lead(jnp.where(listed, pair_block, 0), peers)
        rows_used = pick_lead(jnp.where(listed, pair_row, 0), peers).reshape(slot_count)
        usable = pick_lead(listed.astype(jnp.int32), peers).reshape(slot_count)[:, None, None] > 0

        requested = jnp.stack(send_up([wanted[offset] for offset in range(peer_count)]))
        far = jnp.concatenate(
            send_down([pick_rows(own_synth, requested[offset], blocks) for offset in range(peer_count)]),
            axis=0,
        )
        requested = requested.reshape(slot_count)
        far_y = far[:, :features]
        far_tags = far[:, features]
        slot_x = pick_rows(own_real, rows_used, blocks)
        slot_tags = pick_rows(real_tags, rows_used, blocks)[:, 0]
        cost = slot_costs(slot_x, slot_tags, far_y, far_tags)
        cost_cols = cost / SMOOTH
        cost_rows = jnp.transpose(cost_cols, (0, 2, 1))

        synth_pot = jnp.zeros((marginals, blocks, BLOCK), jnp.float32)
        real_pot = jnp.zeros((marginals, blocks, BLOCK), jnp.float32)
        for sweep_index in range(ITERS):
            if sweep_index == 0:
                panel = jnp.zeros((slot_count, marginals, BLOCK), jnp.float32)
            else:
                panel = jnp.concatenate(
                    send_down(
                        [
                            pick_rows(synth_pot, requested[offset * capacity : (offset + 1) * capacity], blocks)
                            for offset in range(peer_count)
                        ]
                    ),
                    axis=0,
                )
            lse = jnp.where(usable, slot_lse(cost_rows, panel / SMOOTH), SENTINEL)
            block_top, summed = fold_lse(lse, rows_used, blocks)
            block_top, summed = sub_join((block_top, summed))
            real_pot = finish(log_real, block_top, summed)

            own_rows = pick_rows(real_pot, rows_used, blocks)
            lse = jnp.where(usable, slot_lse(cost_cols, own_rows / SMOOTH), SENTINEL)
            back = jnp.concatenate(
                send_up([lse[offset * capacity : (offset + 1) * capacity] for offset in range(peer_count)]),
                axis=0,
            )
            block_top, summed = fold_lse(back, requested, blocks)
            block_top, summed = sub_join((block_top, summed))
            synth_pot = finish(log_synth, block_top, summed)
        return (real_pot.reshape(marginals, point_count), synth_pot.reshape(marginals, point_count))

    return shards


def solution(mesh):
    placed = (
        P(None, ("slab", "blk")),
        P(None, ("slab", "blk")),
        P(("slab", "blk")),
        P(("slab", "blk")),
        P("bag", ("slab", "blk")),
        P("bag", ("slab", "blk")),
        P(("slab", "blk", "sub"), None),
        P(("slab", "blk", "sub"), None),
        P(("slab", "blk", "sub")),
    )
    return jax.shard_map(
        make_shards(mesh.shape["blk"], mesh.shape["sub"]),
        mesh=mesh,
        in_specs=placed,
        out_specs=(P("bag", ("slab", "blk")), P("bag", ("slab", "blk"))),
        check_vma=False,
    )
```

```python
import jax
import jax.numpy as jnp
from jax import lax
from jax.sharding import PartitionSpec as P

BLOCK = 128
ITERS = 2


SMOOTH = 0.1
PENALTY = 0.3
SENTINEL = -1e30


def join_parts(earlier, latter):
    larger = jnp.maximum(earlier[0], latter[0])
    return (
        larger,
        earlier[1] * jnp.exp(earlier[0] - larger) + latter[1] * jnp.exp(latter[0] - larger),
    )


def pick_rows(values, ids, blocks):
    hits = ids[:, None] == jnp.arange(blocks, dtype=jnp.int32)[None, :]
    chosen = jnp.where(hits[:, None, :, None], values[None], jnp.zeros((), values.dtype))
    return jnp.sum(chosen, axis=2, dtype=values.dtype)


def pick_lead(values, ids):
    hits = ids[:, None] == jnp.arange(values.shape[0], dtype=jnp.int32)[None, :]
    hits = hits.reshape(hits.shape + (1,) * (values.ndim - 1))
    return jnp.sum(jnp.where(hits, values[None], jnp.zeros((), values.dtype)), axis=1, dtype=values.dtype)


def fold_blocks(highest, mass_sum, owners, blocks):
    matches = owners[:, None] == jnp.arange(blocks, dtype=jnp.int32)[None, :]
    match_mask = matches[:, None, :, None]
    block_top = jnp.max(jnp.where(match_mask, highest[:, :, None, :], SENTINEL), axis=0)
    slot_top = pick_rows(block_top, owners, blocks)
    scaled = mass_sum * jnp.exp(highest - slot_top)
    summed = jnp.sum(jnp.where(match_mask, scaled[:, :, None, :], 0.0), axis=0)
    return (block_top, summed)


def fold_lse(lse, owners, blocks):
    matches = owners[:, None] == jnp.arange(blocks, dtype=jnp.int32)[None, :]
    match_mask = matches[:, None, :, None]
    block_top = jnp.max(jnp.where(match_mask, lse[:, :, None, :], SENTINEL), axis=0)
    slot_top = pick_rows(block_top, owners, blocks)
    scaled = jnp.where(lse > 0.5 * SENTINEL, jnp.exp(lse - slot_top), 0.0)
    summed = jnp.sum(jnp.where(match_mask, scaled[:, :, None, :], 0.0), axis=0)
    return (block_top, summed)


def finish(log_weight, block_top, summed):
    spread = jnp.where(summed > 0.5, block_top + jnp.log(jnp.maximum(summed, 0.5)), 0.0)
    return SMOOTH * log_weight - SMOOTH * spread


def slot_costs(slot_real, slot_real_tag, slot_synth, slot_synth_tag):
    inner_prod = jnp.einsum(
        "gdi,gdj->gij", slot_real, slot_synth, preferred_element_type=jnp.float32
    )
    real_sq = jnp.sum(jnp.square(slot_real.astype(jnp.float32)), axis=1)
    synth_sq = jnp.sum(jnp.square(slot_synth.astype(jnp.float32)), axis=1)
    differ = (slot_real_tag[:, :, None] != slot_synth_tag[:, None, :]).astype(jnp.float32)
    return 0.5 * real_sq[:, :, None] + 0.5 * synth_sq[:, None, :] - inner_prod + PENALTY * differ


def lse_parts(scores, axis):
    highest = jnp.max(scores, axis=axis)
    mass_sum = jnp.sum(jnp.exp(scores - jnp.expand_dims(highest, axis)), axis=axis)
    return (highest, mass_sum)


def make_shards(n_blk, n_sub):
    def sub_join(parts):
        if n_sub == 2:
            other = lax.ppermute(jnp.stack(parts), "sub", [(0, 1), (1, 0)])
            return join_parts(parts, (other[0], other[1]))
        pieces = lax.all_gather(jnp.stack(parts), "sub")
        subtotal = (pieces[0, 0], pieces[0, 1])
        for index in range(1, n_sub):
            subtotal = join_parts(subtotal, (pieces[index, 0], pieces[index, 1]))
        return subtotal

    def send_up(chunks):
        moved = [chunks[0]]
        for offset in range(1, n_blk):
            perm = [(index, (index + offset) % n_blk) for index in range(n_blk)]
            moved.append(lax.ppermute(chunks[offset], "blk", perm))
        return moved

    def send_down(chunks):
        moved = [chunks[0]]
        for offset in range(1, n_blk):
            perm = [(index, (index - offset) % n_blk) for index in range(n_blk)]
            moved.append(lax.ppermute(chunks[offset], "blk", perm))
        return moved

    def shards(
        real_points,
        synth_points,
        real_cluster,
        synth_cluster,
        real_weight,
        synth_weight,
        pair_block,
        pair_row,
        pair_count,
    ):
        features, point_count = real_points.shape
        blocks = point_count // BLOCK
        marginals = real_weight.shape[0]
        peer_count, capacity = pair_block.shape
        slot_count = peer_count * capacity
        my_blk = lax.axis_index("blk")
        own_real = real_points.reshape(features, blocks, BLOCK)
        real_tags = real_cluster.reshape(1, blocks, BLOCK).astype(jnp.bfloat16)
        own_synth = jnp.concatenate(
            [synth_points, synth_cluster.astype(jnp.bfloat16)[None, :]], axis=0
        ).reshape(features + 1, blocks, BLOCK)
        log_real = jnp.log(real_weight.astype(jnp.float32) + 0.5).reshape(marginals, blocks, BLOCK)
        log_synth = jnp.log(synth_weight.astype(jnp.float32) + 0.5).reshape(marginals, blocks, BLOCK)

        peers = (my_blk + jnp.arange(peer_count, dtype=jnp.int32)) % peer_count
        listed = lax.broadcasted_iota(jnp.int32, (peer_count, capacity), 1) < pair_count[:, None]
        wanted = pick_lead(jnp.where(listed, pair_block, 0), peers)
        rows_used = pick_lead(jnp.where(listed, pair_row, 0), peers).reshape(slot_count)
        usable = pick_lead(listed.astype(jnp.int32), peers).reshape(slot_count)[:, None, None] > 0

        requested = jnp.stack(send_up([wanted[offset] for offset in range(peer_count)]))
        far = jnp.concatenate(
            send_down([pick_rows(own_synth, requested[offset], blocks) for offset in range(peer_count)]),
            axis=0,
        )
        requested = requested.reshape(slot_count)
        far_y = far[:, :features]
        far_tags = far[:, features]
        slot_x = pick_rows(own_real, rows_used, blocks)
        slot_tags = pick_rows(real_tags, rows_used, blocks)[:, 0]
        cost = slot_costs(slot_x, slot_tags, far_y, far_tags)
        cost_cols = cost / SMOOTH
        cost_rows = jnp.transpose(cost_cols, (0, 2, 1))

        synth_pot = jnp.zeros((marginals, blocks, BLOCK), jnp.float32)
        real_pot = jnp.zeros((marginals, blocks, BLOCK), jnp.float32)
        for sweep_index in range(ITERS):
            if sweep_index == 0:
                panel = jnp.zeros((slot_count, 1, BLOCK), jnp.float32)
            else:
                panel = jnp.concatenate(
                    send_down(
                        [
                            pick_rows(synth_pot, requested[offset * capacity : (offset + 1) * capacity], blocks)
                            for offset in range(peer_count)
                        ]
                    ),
                    axis=0,
                )
            scores = (panel / SMOOTH)[:, :, :, None] - cost_rows[:, None]
            highest, mass_sum = lse_parts(scores, 2)
            highest = jnp.where(usable, highest, SENTINEL)
            mass_sum = jnp.where(usable, mass_sum, 0.0)
            block_top, summed = fold_blocks(highest, mass_sum, rows_used, blocks)
            block_top, summed = sub_join((block_top, summed))
            real_pot = finish(log_real, block_top, summed)

            own_rows = pick_rows(real_pot, rows_used, blocks)
            scores = (own_rows / SMOOTH)[:, :, :, None] - cost_cols[:, None]
            highest, mass_sum = lse_parts(scores, 2)
            lse = jnp.where(usable, highest + jnp.log(mass_sum), SENTINEL)
            back = jnp.concatenate(
                send_up([lse[offset * capacity : (offset + 1) * capacity] for offset in range(peer_count)]),
                axis=0,
            )
            block_top, summed = fold_lse(back, requested, blocks)
            block_top, summed = sub_join((block_top, summed))
            synth_pot = finish(log_synth, block_top, summed)
        return (real_pot.reshape(marginals, point_count), synth_pot.reshape(marginals, point_count))

    return shards


def solution(mesh):
    placed = (
        P(None, ("slab", "blk")),
        P(None, ("slab", "blk")),
        P(("slab", "blk")),
        P(("slab", "blk")),
        P("bag", ("slab", "blk")),
        P("bag", ("slab", "blk")),
        P(("slab", "blk", "sub"), None),
        P(("slab", "blk", "sub"), None),
        P(("slab", "blk", "sub")),
    )
    return jax.shard_map(
        make_shards(mesh.shape["blk"], mesh.shape["sub"]),
        mesh=mesh,
        in_specs=placed,
        out_specs=(P("bag", ("slab", "blk")), P("bag", ("slab", "blk"))),
        check_vma=False,
    )
```

```python
import jax
import jax.numpy as jnp
from jax import lax
from jax.sharding import PartitionSpec as P

BLOCK = 128
ITERS = 2


SMOOTH = 0.1
PENALTY = 0.3
SENTINEL = -1e30


def join_parts(earlier, latter):
    larger = jnp.maximum(earlier[0], latter[0])
    return (
        larger,
        earlier[1] * jnp.exp(earlier[0] - larger) + latter[1] * jnp.exp(latter[0] - larger),
    )


def pick_rows(values, ids, blocks):
    hits = ids[:, None] == jnp.arange(blocks, dtype=jnp.int32)[None, :]
    chosen = jnp.where(hits[:, None, :, None], values[None], jnp.zeros((), values.dtype))
    return jnp.sum(chosen, axis=2, dtype=values.dtype)


def pick_lead(values, ids):
    hits = ids[:, None] == jnp.arange(values.shape[0], dtype=jnp.int32)[None, :]
    hits = hits.reshape(hits.shape + (1,) * (values.ndim - 1))
    return jnp.sum(jnp.where(hits, values[None], jnp.zeros((), values.dtype)), axis=1, dtype=values.dtype)


def fold_blocks(highest, mass_sum, owners, blocks):
    matches = owners[:, None] == jnp.arange(blocks, dtype=jnp.int32)[None, :]
    match_mask = matches[:, None, :, None]
    block_top = jnp.max(jnp.where(match_mask, highest[:, :, None, :], SENTINEL), axis=0)
    slot_top = pick_rows(block_top, owners, blocks)
    scaled = mass_sum * jnp.exp(highest - slot_top)
    summed = jnp.sum(jnp.where(match_mask, scaled[:, :, None, :], 0.0), axis=0)
    return (block_top, summed)


def fold_lse(lse, owners, blocks):
    matches = owners[:, None] == jnp.arange(blocks, dtype=jnp.int32)[None, :]
    match_mask = matches[:, None, :, None]
    block_top = jnp.max(jnp.where(match_mask, lse[:, :, None, :], SENTINEL), axis=0)
    slot_top = pick_rows(block_top, owners, blocks)
    scaled = jnp.where(lse > 0.5 * SENTINEL, jnp.exp(lse - slot_top), 0.0)
    summed = jnp.sum(jnp.where(match_mask, scaled[:, :, None, :], 0.0), axis=0)
    return (block_top, summed)


def finish(log_weight, block_top, summed):
    spread = jnp.where(summed > 0.5, block_top + jnp.log(jnp.maximum(summed, 0.5)), 0.0)
    return SMOOTH * log_weight - SMOOTH * spread


def slot_costs(slot_real, slot_real_tag, slot_synth, slot_synth_tag):
    inner_prod = jnp.einsum(
        "gdi,gdj->gij", slot_real, slot_synth, preferred_element_type=jnp.float32
    )
    real_sq = jnp.sum(jnp.square(slot_real.astype(jnp.float32)), axis=1)
    synth_sq = jnp.sum(jnp.square(slot_synth.astype(jnp.float32)), axis=1)
    differ = (slot_real_tag[:, :, None] != slot_synth_tag[:, None, :]).astype(jnp.float32)
    return 0.5 * real_sq[:, :, None] + 0.5 * synth_sq[:, None, :] - inner_prod + PENALTY * differ


def lse_parts(scores, axis):
    highest = jnp.max(scores, axis=axis)
    mass_sum = jnp.sum(jnp.exp(scores - jnp.expand_dims(highest, axis)), axis=axis)
    return (highest, mass_sum)


def make_shards(n_blk, n_sub):
    def swap(value):
        return lax.ppermute(value, "sub", [(0, 1), (1, 0)])

    def send_up(chunks):
        moved = [chunks[0]]
        for offset in range(1, n_blk):
            perm = [(index, (index + offset) % n_blk) for index in range(n_blk)]
            moved.append(lax.ppermute(chunks[offset], "blk", perm))
        return moved

    def send_down(chunks):
        moved = [chunks[0]]
        for offset in range(1, n_blk):
            perm = [(index, (index - offset) % n_blk) for index in range(n_blk)]
            moved.append(lax.ppermute(chunks[offset], "blk", perm))
        return moved

    def shards(
        real_points,
        synth_points,
        real_cluster,
        synth_cluster,
        real_weight,
        synth_weight,
        pair_block,
        pair_row,
        pair_count,
    ):
        features, point_count = real_points.shape
        blocks = point_count // BLOCK
        marginals = real_weight.shape[0]
        half = marginals // n_sub
        peer_count, capacity = pair_block.shape
        wide = n_sub * capacity
        slot_count = peer_count * wide
        my_blk = lax.axis_index("blk")
        my_sub = lax.axis_index("sub")
        own_real = real_points.reshape(features, blocks, BLOCK)
        real_tags = real_cluster.reshape(1, blocks, BLOCK).astype(jnp.bfloat16)
        own_synth = jnp.concatenate(
            [synth_points, synth_cluster.astype(jnp.bfloat16)[None, :]], axis=0
        ).reshape(features + 1, blocks, BLOCK)
        log_real = jnp.log(
            lax.dynamic_slice_in_dim(real_weight, my_sub * half, half, 0).astype(jnp.float32) + 0.5
        ).reshape(half, blocks, BLOCK)
        log_synth = jnp.log(
            lax.dynamic_slice_in_dim(synth_weight, my_sub * half, half, 0).astype(jnp.float32) + 0.5
        ).reshape(half, blocks, BLOCK)

        peers = (my_blk + jnp.arange(peer_count, dtype=jnp.int32)) % peer_count
        lists = jnp.stack([pair_block, pair_row, jnp.broadcast_to(pair_count[:, None], pair_block.shape)])
        lists = jnp.stack([lists, swap(lists)], axis=1)
        listed = lax.broadcasted_iota(jnp.int32, lists.shape[1:], 2) < lists[2]
        wanted = pick_lead(jnp.transpose(jnp.where(listed, lists[0], 0), (1, 0, 2)), peers)
        rows_used = pick_lead(jnp.transpose(jnp.where(listed, lists[1], 0), (1, 0, 2)), peers)
        usable = pick_lead(jnp.transpose(listed.astype(jnp.int32), (1, 0, 2)), peers)
        rows_used = rows_used.reshape(slot_count)
        usable = usable.reshape(slot_count)[:, None, None] > 0

        requested = jnp.stack(send_up([wanted[offset, 0] for offset in range(peer_count)]))
        far = jnp.stack(
            send_down([pick_rows(own_synth, requested[offset], blocks) for offset in range(peer_count)])
        )
        requested = jnp.stack([requested, swap(requested)], axis=1).reshape(slot_count)
        far = jnp.stack([far, swap(far)], axis=1).reshape(slot_count, features + 1, BLOCK)
        far_y = far[:, :features]
        far_tags = far[:, features]
        slot_x = pick_rows(own_real, rows_used, blocks)
        slot_tags = pick_rows(real_tags, rows_used, blocks)[:, 0]
        cost = slot_costs(slot_x, slot_tags, far_y, far_tags)
        cost_cols = cost / SMOOTH
        cost_rows = jnp.transpose(cost_cols, (0, 2, 1))

        synth_pot = jnp.zeros((half, blocks, BLOCK), jnp.float32)
        real_pot = jnp.zeros((half, blocks, BLOCK), jnp.float32)
        for sweep_index in range(ITERS):
            if sweep_index == 0:
                panel = jnp.zeros((slot_count, 1, BLOCK), jnp.float32)
            else:
                panel = jnp.concatenate(
                    send_down(
                        [
                            pick_rows(synth_pot, requested[offset * wide : (offset + 1) * wide], blocks)
                            for offset in range(peer_count)
                        ]
                    ),
                    axis=0,
                )
            scores = (panel / SMOOTH)[:, :, :, None] - cost_rows[:, None]
            highest, mass_sum = lse_parts(scores, 2)
            highest = jnp.where(usable, highest, SENTINEL)
            mass_sum = jnp.where(usable, mass_sum, 0.0)
            block_top, summed = fold_blocks(highest, mass_sum, rows_used, blocks)
            real_pot = finish(log_real, block_top, summed)

            own_rows = pick_rows(real_pot, rows_used, blocks)
            scores = (own_rows / SMOOTH)[:, :, :, None] - cost_cols[:, None]
            highest, mass_sum = lse_parts(scores, 2)
            lse = jnp.where(usable, highest + jnp.log(mass_sum), SENTINEL)
            back = jnp.concatenate(
                send_up([lse[offset * wide : (offset + 1) * wide] for offset in range(peer_count)]),
                axis=0,
            )
            block_top, summed = fold_lse(back, requested, blocks)
            synth_pot = finish(log_synth, block_top, summed)

        def both_halves(mine):
            other = swap(mine)
            first = jnp.where(my_sub == 0, mine, other)
            second = jnp.where(my_sub == 0, other, mine)
            return jnp.concatenate([first, second], axis=0).reshape(marginals, point_count)

        return (both_halves(real_pot), both_halves(synth_pot))

    return shards


def solution(mesh):
    placed = (
        P(None, ("slab", "blk")),
        P(None, ("slab", "blk")),
        P(("slab", "blk")),
        P(("slab", "blk")),
        P("bag", ("slab", "blk")),
        P("bag", ("slab", "blk")),
        P(("slab", "blk", "sub"), None),
        P(("slab", "blk", "sub"), None),
        P(("slab", "blk", "sub")),
    )
    return jax.shard_map(
        make_shards(mesh.shape["blk"], mesh.shape["sub"]),
        mesh=mesh,
        in_specs=placed,
        out_specs=(P("bag", ("slab", "blk")), P("bag", ("slab", "blk"))),
        check_vma=False,
    )
```

```python
import jax
import jax.numpy as jnp
from jax import lax
from jax.sharding import PartitionSpec as P

BLOCK = 128
ITERS = 2


SMOOTH = 0.1
PENALTY = 0.3
SENTINEL = -1e30


def join_parts(earlier, latter):
    larger = jnp.maximum(earlier[0], latter[0])
    return (
        larger,
        earlier[1] * jnp.exp(earlier[0] - larger) + latter[1] * jnp.exp(latter[0] - larger),
    )


def pick_rows(values, ids, blocks):
    hits = ids[:, None] == jnp.arange(blocks, dtype=jnp.int32)[None, :]
    chosen = jnp.where(hits[:, None, :, None], values[None], jnp.zeros((), values.dtype))
    return jnp.sum(chosen, axis=2, dtype=values.dtype)


def pick_lead(values, ids):
    hits = ids[:, None] == jnp.arange(values.shape[0], dtype=jnp.int32)[None, :]
    hits = hits.reshape(hits.shape + (1,) * (values.ndim - 1))
    return jnp.sum(jnp.where(hits, values[None], jnp.zeros((), values.dtype)), axis=1, dtype=values.dtype)


def fold_blocks(highest, mass_sum, owners, blocks):
    matches = owners[:, None] == jnp.arange(blocks, dtype=jnp.int32)[None, :]
    match_mask = matches[:, None, :, None]
    block_top = jnp.max(jnp.where(match_mask, highest[:, :, None, :], SENTINEL), axis=0)
    slot_top = pick_rows(block_top, owners, blocks)
    scaled = mass_sum * jnp.exp(highest - slot_top)
    summed = jnp.sum(jnp.where(match_mask, scaled[:, :, None, :], 0.0), axis=0)
    return (block_top, summed)


def fold_lse(lse, owners, blocks):
    matches = owners[:, None] == jnp.arange(blocks, dtype=jnp.int32)[None, :]
    match_mask = matches[:, None, :, None]
    block_top = jnp.max(jnp.where(match_mask, lse[:, :, None, :], SENTINEL), axis=0)
    slot_top = pick_rows(block_top, owners, blocks)
    scaled = jnp.where(lse > 0.5 * SENTINEL, jnp.exp(lse - slot_top), 0.0)
    summed = jnp.sum(jnp.where(match_mask, scaled[:, :, None, :], 0.0), axis=0)
    return (block_top, summed)


def finish(log_weight, block_top, summed):
    spread = jnp.where(summed > 0.5, block_top + jnp.log(jnp.maximum(summed, 0.5)), 0.0)
    return SMOOTH * log_weight - SMOOTH * spread


def slot_costs(slot_real, slot_real_tag, slot_synth, slot_synth_tag):
    inner_prod = jnp.einsum(
        "gdi,gdj->gij", slot_real, slot_synth, preferred_element_type=jnp.float32
    )
    real_sq = jnp.sum(jnp.square(slot_real.astype(jnp.float32)), axis=1)
    synth_sq = jnp.sum(jnp.square(slot_synth.astype(jnp.float32)), axis=1)
    differ = (slot_real_tag[:, :, None] != slot_synth_tag[:, None, :]).astype(jnp.float32)
    return 0.5 * real_sq[:, :, None] + 0.5 * synth_sq[:, None, :] - inner_prod + PENALTY * differ


def lse_parts(scores, axis):
    highest = jnp.max(scores, axis=axis)
    mass_sum = jnp.sum(jnp.exp(scores - jnp.expand_dims(highest, axis)), axis=axis)
    return (highest, mass_sum)


def make_shards(n_blk, n_sub):
    def swap(value):
        return lax.ppermute(value, "sub", [(0, 1), (1, 0)])

    def send_up(chunks):
        moved = [chunks[0]]
        for offset in range(1, n_blk):
            perm = [(index, (index + offset) % n_blk) for index in range(n_blk)]
            moved.append(lax.ppermute(chunks[offset], "blk", perm))
        return moved

    def send_down(chunks):
        moved = [chunks[0]]
        for offset in range(1, n_blk):
            perm = [(index, (index - offset) % n_blk) for index in range(n_blk)]
            moved.append(lax.ppermute(chunks[offset], "blk", perm))
        return moved

    def shards(
        real_points,
        synth_points,
        real_cluster,
        synth_cluster,
        real_weight,
        synth_weight,
        pair_block,
        pair_row,
        pair_count,
    ):
        features, point_count = real_points.shape
        blocks = point_count // BLOCK
        marginals = real_weight.shape[0]
        half = marginals // n_sub
        peer_count, capacity = pair_block.shape
        wide = n_sub * capacity
        slot_count = peer_count * wide
        my_blk = lax.axis_index("blk")
        my_sub = lax.axis_index("sub")
        own_real = real_points.reshape(features, blocks, BLOCK)
        real_tags = real_cluster.reshape(1, blocks, BLOCK).astype(jnp.bfloat16)
        own_synth = jnp.concatenate(
            [synth_points, synth_cluster.astype(jnp.bfloat16)[None, :]], axis=0
        ).reshape(features + 1, blocks, BLOCK)
        log_real = jnp.log(
            lax.dynamic_slice_in_dim(real_weight, my_sub * half, half, 0).astype(jnp.float32) + 0.5
        ).reshape(half, blocks, BLOCK)
        log_synth = jnp.log(
            lax.dynamic_slice_in_dim(synth_weight, my_sub * half, half, 0).astype(jnp.float32) + 0.5
        ).reshape(half, blocks, BLOCK)

        peers = (my_blk + jnp.arange(peer_count, dtype=jnp.int32)) % peer_count
        own_listed = lax.broadcasted_iota(jnp.int32, (peer_count, capacity), 1) < pair_count[:, None]
        own_wanted = pick_lead(jnp.where(own_listed, pair_block, 0), peers)
        requested = jnp.stack(send_up([own_wanted[offset] for offset in range(peer_count)]))
        lists = jnp.stack([pair_block, pair_row, jnp.broadcast_to(pair_count[:, None], pair_block.shape)])
        lists = jnp.stack([lists, swap(lists)], axis=1)
        listed = lax.broadcasted_iota(jnp.int32, lists.shape[1:], 2) < lists[2]
        rows_used = pick_lead(jnp.transpose(jnp.where(listed, lists[1], 0), (1, 0, 2)), peers)
        usable = pick_lead(jnp.transpose(listed.astype(jnp.int32), (1, 0, 2)), peers)
        rows_used = rows_used.reshape(slot_count)
        usable = usable.reshape(slot_count)[:, None, None] > 0

        far = jnp.stack(
            send_down([pick_rows(own_synth, requested[offset], blocks) for offset in range(peer_count)])
        )
        requested = jnp.stack([requested, swap(requested)], axis=1).reshape(slot_count)
        far = jnp.stack([far, swap(far)], axis=1).reshape(slot_count, features + 1, BLOCK)
        far_y = far[:, :features]
        far_tags = far[:, features]
        slot_x = pick_rows(own_real, rows_used, blocks)
        slot_tags = pick_rows(real_tags, rows_used, blocks)[:, 0]
        cost_cols = slot_costs(slot_x, slot_tags, far_y, far_tags) / SMOOTH
        cost_rows = slot_costs(far_y, far_tags, slot_x, slot_tags) / SMOOTH

        synth_pot = jnp.zeros((half, blocks, BLOCK), jnp.float32)
        real_pot = jnp.zeros((half, blocks, BLOCK), jnp.float32)
        for sweep_index in range(ITERS):
            if sweep_index == 0:
                panel = jnp.zeros((slot_count, 1, BLOCK), jnp.float32)
            else:
                panel = jnp.concatenate(
                    send_down(
                        [
                            pick_rows(synth_pot, requested[offset * wide : (offset + 1) * wide], blocks)
                            for offset in range(peer_count)
                        ]
                    ),
                    axis=0,
                )
            scores = (panel / SMOOTH)[:, :, :, None] - cost_rows[:, None]
            highest, mass_sum = lse_parts(scores, 2)
            highest = jnp.where(usable, highest, SENTINEL)
            mass_sum = jnp.where(usable, mass_sum, 0.0)
            block_top, summed = fold_blocks(highest, mass_sum, rows_used, blocks)
            real_pot = finish(log_real, block_top, summed)

            own_rows = pick_rows(real_pot, rows_used, blocks)
            scores = (own_rows / SMOOTH)[:, :, :, None] - cost_cols[:, None]
            highest, mass_sum = lse_parts(scores, 2)
            lse = jnp.where(usable, highest + jnp.log(mass_sum), SENTINEL)
            back = jnp.concatenate(
                send_up([lse[offset * wide : (offset + 1) * wide] for offset in range(peer_count)]),
                axis=0,
            )
            block_top, summed = fold_lse(back, requested, blocks)
            synth_pot = finish(log_synth, block_top, summed)

        def both_halves(mine):
            other = swap(mine)
            first = jnp.where(my_sub == 0, mine, other)
            second = jnp.where(my_sub == 0, other, mine)
            return jnp.concatenate([first, second], axis=0).reshape(marginals, point_count)

        return (both_halves(real_pot), both_halves(synth_pot))

    return shards


def solution(mesh):
    placed = (
        P(None, ("slab", "blk")),
        P(None, ("slab", "blk")),
        P(("slab", "blk")),
        P(("slab", "blk")),
        P("bag", ("slab", "blk")),
        P("bag", ("slab", "blk")),
        P(("slab", "blk", "sub"), None),
        P(("slab", "blk", "sub"), None),
        P(("slab", "blk", "sub")),
    )
    return jax.shard_map(
        make_shards(mesh.shape["blk"], mesh.shape["sub"]),
        mesh=mesh,
        in_specs=placed,
        out_specs=(P("bag", ("slab", "blk")), P("bag", ("slab", "blk"))),
        check_vma=False,
    )
```

```python
import jax
import jax.numpy as jnp
from jax import lax
from jax.sharding import PartitionSpec as P

BLOCK = 128
ITERS = 2


SMOOTH = 0.1
PENALTY = 0.3
SENTINEL = -1e30


def join_parts(earlier, latter):
    larger = jnp.maximum(earlier[0], latter[0])
    return (
        larger,
        earlier[1] * jnp.exp(earlier[0] - larger) + latter[1] * jnp.exp(latter[0] - larger),
    )


def pick_rows(values, ids, blocks):
    hits = ids[:, None] == jnp.arange(blocks, dtype=jnp.int32)[None, :]
    chosen = jnp.where(hits[:, None, :, None], values[None], jnp.zeros((), values.dtype))
    return jnp.sum(chosen, axis=2, dtype=values.dtype)


def pick_lead(values, ids):
    hits = ids[:, None] == jnp.arange(values.shape[0], dtype=jnp.int32)[None, :]
    hits = hits.reshape(hits.shape + (1,) * (values.ndim - 1))
    return jnp.sum(jnp.where(hits, values[None], jnp.zeros((), values.dtype)), axis=1, dtype=values.dtype)


def fold_blocks(highest, mass_sum, owners, blocks):
    matches = owners[:, None] == jnp.arange(blocks, dtype=jnp.int32)[None, :]
    match_mask = matches[:, None, :, None]
    block_top = jnp.max(jnp.where(match_mask, highest[:, :, None, :], SENTINEL), axis=0)
    slot_top = pick_rows(block_top, owners, blocks)
    scaled = mass_sum * jnp.exp(highest - slot_top)
    summed = jnp.sum(jnp.where(match_mask, scaled[:, :, None, :], 0.0), axis=0)
    return (block_top, summed)


def fold_lse(lse, owners, blocks):
    matches = owners[:, None] == jnp.arange(blocks, dtype=jnp.int32)[None, :]
    match_mask = matches[:, None, :, None]
    block_top = jnp.max(jnp.where(match_mask, lse[:, :, None, :], SENTINEL), axis=0)
    slot_top = pick_rows(block_top, owners, blocks)
    scaled = jnp.where(lse > 0.5 * SENTINEL, jnp.exp(lse - slot_top), 0.0)
    summed = jnp.sum(jnp.where(match_mask, scaled[:, :, None, :], 0.0), axis=0)
    return (block_top, summed)


def finish(log_weight, block_top, summed):
    spread = jnp.where(summed > 0.5, block_top + jnp.log(jnp.maximum(summed, 0.5)), 0.0)
    return SMOOTH * log_weight - SMOOTH * spread


def slot_costs(slot_real, slot_real_tag, slot_synth, slot_synth_tag):
    inner_prod = jnp.einsum(
        "gdi,gdj->gij", slot_real, slot_synth, preferred_element_type=jnp.float32
    )
    real_sq = jnp.sum(jnp.square(slot_real.astype(jnp.float32)), axis=1)
    synth_sq = jnp.sum(jnp.square(slot_synth.astype(jnp.float32)), axis=1)
    differ = (slot_real_tag[:, :, None] != slot_synth_tag[:, None, :]).astype(jnp.float32)
    return 0.5 * real_sq[:, :, None] + 0.5 * synth_sq[:, None, :] - inner_prod + PENALTY * differ


def lse_parts(scores, axis):
    highest = jnp.max(scores, axis=axis)
    mass_sum = jnp.sum(jnp.exp(scores - jnp.expand_dims(highest, axis)), axis=axis)
    return (highest, mass_sum)


def make_shards(n_blk, n_sub):
    def swap(value):
        return lax.ppermute(value, "sub", [(0, 1), (1, 0)])

    def send_up(chunks):
        moved = [chunks[0]]
        for offset in range(1, n_blk):
            perm = [(index, (index + offset) % n_blk) for index in range(n_blk)]
            moved.append(lax.ppermute(chunks[offset], "blk", perm))
        return moved

    def send_down(chunks):
        moved = [chunks[0]]
        for offset in range(1, n_blk):
            perm = [(index, (index - offset) % n_blk) for index in range(n_blk)]
            moved.append(lax.ppermute(chunks[offset], "blk", perm))
        return moved

    def shards(
        real_points,
        synth_points,
        real_cluster,
        synth_cluster,
        real_weight,
        synth_weight,
        pair_block,
        pair_row,
        pair_count,
    ):
        features, point_count = real_points.shape
        blocks = point_count // BLOCK
        marginals = real_weight.shape[0]
        half = marginals // n_sub
        peer_count, capacity = pair_block.shape
        wide = n_sub * capacity
        slot_count = peer_count * wide
        my_blk = lax.axis_index("blk")
        my_sub = lax.axis_index("sub")
        own_real = real_points.reshape(features, blocks, BLOCK)
        real_tags = real_cluster.reshape(1, blocks, BLOCK).astype(jnp.bfloat16)
        own_synth = jnp.concatenate(
            [synth_points, synth_cluster.astype(jnp.bfloat16)[None, :]], axis=0
        ).reshape(features + 1, blocks, BLOCK)
        log_real = jnp.log(
            lax.dynamic_slice_in_dim(real_weight, my_sub * half, half, 0).astype(jnp.float32) + 0.5
        ).reshape(half, blocks, BLOCK)
        log_synth = jnp.log(
            lax.dynamic_slice_in_dim(synth_weight, my_sub * half, half, 0).astype(jnp.float32) + 0.5
        ).reshape(half, blocks, BLOCK)

        peers = (my_blk + jnp.arange(peer_count, dtype=jnp.int32)) % peer_count
        everything = send_down([own_synth] * peer_count)
        lists = jnp.stack([pair_block, pair_row, jnp.broadcast_to(pair_count[:, None], pair_block.shape)])
        lists = jnp.stack([lists, swap(lists)], axis=1)
        listed = lax.broadcasted_iota(jnp.int32, lists.shape[1:], 2) < lists[2]
        wanted = pick_lead(jnp.transpose(jnp.where(listed, lists[0], 0), (1, 0, 2)), peers)
        rows_used = pick_lead(jnp.transpose(jnp.where(listed, lists[1], 0), (1, 0, 2)), peers)
        usable = pick_lead(jnp.transpose(listed.astype(jnp.int32), (1, 0, 2)), peers)
        wanted = wanted.reshape(peer_count, wide)
        rows_used = rows_used.reshape(slot_count)
        usable = usable.reshape(slot_count)[:, None, None] > 0
        far = jnp.concatenate(
            [pick_rows(everything[offset], wanted[offset], blocks) for offset in range(peer_count)], axis=0
        )
        far_y = far[:, :features]
        far_tags = far[:, features]
        slot_x = pick_rows(own_real, rows_used, blocks)
        slot_tags = pick_rows(real_tags, rows_used, blocks)[:, 0]
        cost_cols = slot_costs(slot_x, slot_tags, far_y, far_tags) / SMOOTH
        cost_rows = slot_costs(far_y, far_tags, slot_x, slot_tags) / SMOOTH

        synth_pot = jnp.zeros((half, blocks, BLOCK), jnp.float32)
        real_pot = jnp.zeros((half, blocks, BLOCK), jnp.float32)
        for sweep_index in range(ITERS):
            if sweep_index == 0:
                panel = jnp.zeros((slot_count, 1, BLOCK), jnp.float32)
            else:
                panel = jnp.concatenate(
                    send_down(
                        [
                            pick_rows(synth_pot, requested[offset * wide : (offset + 1) * wide], blocks)
                            for offset in range(peer_count)
                        ]
                    ),
                    axis=0,
                )
            scores = (panel / SMOOTH)[:, :, :, None] - cost_rows[:, None]
            highest, mass_sum = lse_parts(scores, 2)
            highest = jnp.where(usable, highest, SENTINEL)
            mass_sum = jnp.where(usable, mass_sum, 0.0)
            block_top, summed = fold_blocks(highest, mass_sum, rows_used, blocks)
            real_pot = finish(log_real, block_top, summed)

            own_rows = pick_rows(real_pot, rows_used, blocks)
            scores = (own_rows / SMOOTH)[:, :, :, None] - cost_cols[:, None]
            highest, mass_sum = lse_parts(scores, 2)
            lse = jnp.where(usable, highest + jnp.log(mass_sum), SENTINEL)
            if sweep_index == 0:
                block_ids = jnp.broadcast_to(wanted.reshape(slot_count, 1, 1).astype(jnp.float32), (slot_count, 1, BLOCK))
                lse = jnp.concatenate([lse, block_ids], axis=1)
            back = jnp.concatenate(
                send_up([lse[offset * wide : (offset + 1) * wide] for offset in range(peer_count)]),
                axis=0,
            )
            if sweep_index == 0:
                requested = back[:, half, 0].astype(jnp.int32)
                back = back[:, :half]
            block_top, summed = fold_lse(back, requested, blocks)
            synth_pot = finish(log_synth, block_top, summed)

        def both_halves(mine):
            other = swap(mine)
            first = jnp.where(my_sub == 0, mine, other)
            second = jnp.where(my_sub == 0, other, mine)
            return jnp.concatenate([first, second], axis=0).reshape(marginals, point_count)

        return (both_halves(real_pot), both_halves(synth_pot))

    return shards


def solution(mesh):
    placed = (
        P(None, ("slab", "blk")),
        P(None, ("slab", "blk")),
        P(("slab", "blk")),
        P(("slab", "blk")),
        P("bag", ("slab", "blk")),
        P("bag", ("slab", "blk")),
        P(("slab", "blk", "sub"), None),
        P(("slab", "blk", "sub"), None),
        P(("slab", "blk", "sub")),
    )
    return jax.shard_map(
        make_shards(mesh.shape["blk"], mesh.shape["sub"]),
        mesh=mesh,
        in_specs=placed,
        out_specs=(P("bag", ("slab", "blk")), P("bag", ("slab", "blk"))),
        check_vma=False,
    )
```

```python
import jax
import jax.numpy as jnp
from jax import lax
from jax.sharding import PartitionSpec as P

BLOCK = 128
ITERS = 2


SMOOTH = 0.1
PENALTY = 0.3
SENTINEL = -1e30


def join_parts(earlier, latter):
    larger = jnp.maximum(earlier[0], latter[0])
    return (
        larger,
        earlier[1] * jnp.exp(earlier[0] - larger) + latter[1] * jnp.exp(latter[0] - larger),
    )


def pick_rows(values, ids, blocks):
    hits = ids[:, None] == jnp.arange(blocks, dtype=jnp.int32)[None, :]
    chosen = jnp.where(hits[:, None, :, None], values[None], jnp.zeros((), values.dtype))
    return jnp.sum(chosen, axis=2, dtype=values.dtype)


def pick_lead(values, ids):
    hits = ids[:, None] == jnp.arange(values.shape[0], dtype=jnp.int32)[None, :]
    hits = hits.reshape(hits.shape + (1,) * (values.ndim - 1))
    return jnp.sum(jnp.where(hits, values[None], jnp.zeros((), values.dtype)), axis=1, dtype=values.dtype)


def fold_blocks(highest, mass_sum, owners, blocks):
    matches = owners[:, None] == jnp.arange(blocks, dtype=jnp.int32)[None, :]
    match_mask = matches[:, None, :, None]
    block_top = jnp.max(jnp.where(match_mask, highest[:, :, None, :], SENTINEL), axis=0)
    slot_top = pick_rows(block_top, owners, blocks)
    scaled = mass_sum * jnp.exp(highest - slot_top)
    summed = jnp.sum(jnp.where(match_mask, scaled[:, :, None, :], 0.0), axis=0)
    return (block_top, summed)


def fold_lse(lse, owners, blocks):
    matches = owners[:, None] == jnp.arange(blocks, dtype=jnp.int32)[None, :]
    match_mask = matches[:, None, :, None]
    block_top = jnp.max(jnp.where(match_mask, lse[:, :, None, :], SENTINEL), axis=0)
    slot_top = pick_rows(block_top, owners, blocks)
    scaled = jnp.where(lse > 0.5 * SENTINEL, jnp.exp(lse - slot_top), 0.0)
    summed = jnp.sum(jnp.where(match_mask, scaled[:, :, None, :], 0.0), axis=0)
    return (block_top, summed)


def finish(log_weight, block_top, summed):
    spread = jnp.where(summed > 0.5, block_top + jnp.log(jnp.maximum(summed, 0.5)), 0.0)
    return SMOOTH * log_weight - SMOOTH * spread


def slot_costs(slot_real, slot_real_tag, slot_synth, slot_synth_tag):
    inner_prod = jnp.einsum(
        "gdi,gdj->gij", slot_real, slot_synth, preferred_element_type=jnp.float32
    )
    real_sq = jnp.sum(jnp.square(slot_real.astype(jnp.float32)), axis=1)
    synth_sq = jnp.sum(jnp.square(slot_synth.astype(jnp.float32)), axis=1)
    differ = (slot_real_tag[:, :, None] != slot_synth_tag[:, None, :]).astype(jnp.float32)
    return 0.5 * real_sq[:, :, None] + 0.5 * synth_sq[:, None, :] - inner_prod + PENALTY * differ


def lse_parts(scores, axis):
    highest = jnp.max(scores, axis=axis)
    mass_sum = jnp.sum(jnp.exp(scores - jnp.expand_dims(highest, axis)), axis=axis)
    return (highest, mass_sum)


def make_shards(n_blk, n_sub):
    def swap(value):
        return lax.ppermute(value, "sub", [(0, 1), (1, 0)])

    def send_up(chunks):
        moved = [chunks[0]]
        for offset in range(1, n_blk):
            perm = [(index, (index + offset) % n_blk) for index in range(n_blk)]
            moved.append(lax.ppermute(chunks[offset], "blk", perm))
        return moved

    def send_down(chunks):
        moved = [chunks[0]]
        for offset in range(1, n_blk):
            perm = [(index, (index - offset) % n_blk) for index in range(n_blk)]
            moved.append(lax.ppermute(chunks[offset], "blk", perm))
        return moved

    def shards(
        real_points,
        synth_points,
        real_cluster,
        synth_cluster,
        real_weight,
        synth_weight,
        pair_block,
        pair_row,
        pair_count,
    ):
        features, point_count = real_points.shape
        blocks = point_count // BLOCK
        marginals = real_weight.shape[0]
        half = marginals // n_sub
        peer_count, capacity = pair_block.shape
        wide = n_sub * capacity
        slot_count = peer_count * wide
        my_blk = lax.axis_index("blk")
        my_sub = lax.axis_index("sub")
        own_real = real_points.reshape(features, blocks, BLOCK)
        real_tags = real_cluster.reshape(1, blocks, BLOCK).astype(jnp.bfloat16)
        own_synth = jnp.concatenate(
            [synth_points, synth_cluster.astype(jnp.bfloat16)[None, :]], axis=0
        ).reshape(features + 1, blocks, BLOCK)
        log_real = jnp.log(
            lax.dynamic_slice_in_dim(real_weight, my_sub * half, half, 0).astype(jnp.float32) + 0.5
        ).reshape(half, blocks, BLOCK)
        log_synth = jnp.log(
            lax.dynamic_slice_in_dim(synth_weight, my_sub * half, half, 0).astype(jnp.float32) + 0.5
        ).reshape(half, blocks, BLOCK)

        peers = (my_blk + jnp.arange(peer_count, dtype=jnp.int32)) % peer_count
        everything = send_down([own_synth] * peer_count)
        lists = jnp.stack([pair_block, pair_row, jnp.broadcast_to(pair_count[:, None], pair_block.shape)])
        lists = jnp.stack([lists, swap(lists)], axis=1)
        listed = lax.broadcasted_iota(jnp.int32, lists.shape[1:], 2) < lists[2]
        wanted = pick_lead(jnp.transpose(jnp.where(listed, lists[0], 0), (1, 0, 2)), peers)
        rows_used = pick_lead(jnp.transpose(jnp.where(listed, lists[1], 0), (1, 0, 2)), peers)
        usable = pick_lead(jnp.transpose(listed.astype(jnp.int32), (1, 0, 2)), peers)
        wanted = wanted.reshape(peer_count, wide)
        rows_used = rows_used.reshape(slot_count)
        usable = usable.reshape(slot_count)[:, None, None] > 0
        far = jnp.concatenate(
            [pick_rows(everything[offset], wanted[offset], blocks) for offset in range(peer_count)], axis=0
        )
        far_y = far[:, :features]
        far_tags = far[:, features]
        slot_x = pick_rows(own_real, rows_used, blocks)
        slot_tags = pick_rows(real_tags, rows_used, blocks)[:, 0]
        cost_cols = slot_costs(slot_x, slot_tags, far_y, far_tags) / SMOOTH
        cost_rows = slot_costs(far_y, far_tags, slot_x, slot_tags) / SMOOTH

        synth_pot = jnp.zeros((half, blocks, BLOCK), jnp.float32)
        real_pot = jnp.zeros((half, blocks, BLOCK), jnp.float32)
        for sweep_index in range(ITERS):
            if sweep_index == 0:
                panel = jnp.zeros((slot_count, 1, BLOCK), jnp.float32)
            else:
                panel = jnp.concatenate(
                    send_down(
                        [
                            pick_rows(synth_pot, requested[offset * wide : (offset + 1) * wide], blocks)
                            for offset in range(peer_count)
                        ]
                    ),
                    axis=0,
                )
            highest, mass_sum = [], []
            for offset in range(peer_count):
                piece = slice(offset * wide, (offset + 1) * wide)
                scores = (panel[piece] / SMOOTH)[:, :, :, None] - cost_rows[piece, None]
                parts = lse_parts(scores, 2)
                highest.append(parts[0])
                mass_sum.append(parts[1])
            highest = jnp.concatenate(highest, axis=0)
            mass_sum = jnp.concatenate(mass_sum, axis=0)
            highest = jnp.where(usable, highest, SENTINEL)
            mass_sum = jnp.where(usable, mass_sum, 0.0)
            block_top, summed = fold_blocks(highest, mass_sum, rows_used, blocks)
            real_pot = finish(log_real, block_top, summed)

            own_rows = pick_rows(real_pot, rows_used, blocks)
            chunks = [None] * peer_count
            for offset in list(range(1, peer_count)) + [0]:
                piece = slice(offset * wide, (offset + 1) * wide)
                scores = (own_rows[piece] / SMOOTH)[:, :, :, None] - cost_cols[piece, None]
                highest, mass_sum = lse_parts(scores, 2)
                lse = jnp.where(usable[piece], highest + jnp.log(mass_sum), SENTINEL)
                if sweep_index == 0:
                    block_ids = jnp.broadcast_to(
                        wanted[offset].reshape(wide, 1, 1).astype(jnp.float32), (wide, 1, BLOCK)
                    )
                    lse = jnp.concatenate([lse, block_ids], axis=1)
                chunks[offset] = lse
            back = jnp.concatenate(send_up(chunks), axis=0)
            if sweep_index == 0:
                requested = back[:, half, 0].astype(jnp.int32)
                back = back[:, :half]
            block_top, summed = fold_lse(back, requested, blocks)
            synth_pot = finish(log_synth, block_top, summed)

        def both_halves(mine):
            other = swap(mine)
            first = jnp.where(my_sub == 0, mine, other)
            second = jnp.where(my_sub == 0, other, mine)
            return jnp.concatenate([first, second], axis=0).reshape(marginals, point_count)

        return (both_halves(real_pot), both_halves(synth_pot))

    return shards


def solution(mesh):
    placed = (
        P(None, ("slab", "blk")),
        P(None, ("slab", "blk")),
        P(("slab", "blk")),
        P(("slab", "blk")),
        P("bag", ("slab", "blk")),
        P("bag", ("slab", "blk")),
        P(("slab", "blk", "sub"), None),
        P(("slab", "blk", "sub"), None),
        P(("slab", "blk", "sub")),
    )
    return jax.shard_map(
        make_shards(mesh.shape["blk"], mesh.shape["sub"]),
        mesh=mesh,
        in_specs=placed,
        out_specs=(P("bag", ("slab", "blk")), P("bag", ("slab", "blk"))),
        check_vma=False,
    )
```

```python
import jax
import jax.numpy as jnp
from jax import lax
from jax.sharding import PartitionSpec as P

BLOCK = 128
ITERS = 2


SMOOTH = 0.1
PENALTY = 0.3
SENTINEL = -1e30


def join_parts(earlier, latter):
    larger = jnp.maximum(earlier[0], latter[0])
    return (
        larger,
        earlier[1] * jnp.exp(earlier[0] - larger) + latter[1] * jnp.exp(latter[0] - larger),
    )


def pick_rows(values, ids, blocks):
    hits = ids[:, None] == jnp.arange(blocks, dtype=jnp.int32)[None, :]
    chosen = jnp.where(hits[:, None, :, None], values[None], jnp.zeros((), values.dtype))
    return jnp.sum(chosen, axis=2, dtype=values.dtype)


def pick_lead(values, ids):
    hits = ids[:, None] == jnp.arange(values.shape[0], dtype=jnp.int32)[None, :]
    hits = hits.reshape(hits.shape + (1,) * (values.ndim - 1))
    return jnp.sum(jnp.where(hits, values[None], jnp.zeros((), values.dtype)), axis=1, dtype=values.dtype)


def fold_blocks(highest, mass_sum, owners, blocks):
    matches = owners[:, None] == jnp.arange(blocks, dtype=jnp.int32)[None, :]
    match_mask = matches[:, None, :, None]
    block_top = jnp.max(jnp.where(match_mask, highest[:, :, None, :], SENTINEL), axis=0)
    slot_top = pick_rows(block_top, owners, blocks)
    scaled = mass_sum * jnp.exp(highest - slot_top)
    summed = jnp.sum(jnp.where(match_mask, scaled[:, :, None, :], 0.0), axis=0)
    return (block_top, summed)


def fold_lse(lse, owners, blocks):
    matches = owners[:, None] == jnp.arange(blocks, dtype=jnp.int32)[None, :]
    match_mask = matches[:, None, :, None]
    block_top = jnp.max(jnp.where(match_mask, lse[:, :, None, :], SENTINEL), axis=0)
    slot_top = pick_rows(block_top, owners, blocks)
    scaled = jnp.where(lse > 0.5 * SENTINEL, jnp.exp(lse - slot_top), 0.0)
    summed = jnp.sum(jnp.where(match_mask, scaled[:, :, None, :], 0.0), axis=0)
    return (block_top, summed)


def finish(log_weight, block_top, summed):
    spread = jnp.where(summed > 0.5, block_top + jnp.log(jnp.maximum(summed, 0.5)), 0.0)
    return SMOOTH * log_weight - SMOOTH * spread


def slot_costs(slot_real, slot_real_tag, slot_synth, slot_synth_tag):
    inner_prod = jnp.einsum(
        "gdi,gdj->gij", slot_real, slot_synth, preferred_element_type=jnp.float32
    )
    real_sq = jnp.sum(jnp.square(slot_real.astype(jnp.float32)), axis=1)
    synth_sq = jnp.sum(jnp.square(slot_synth.astype(jnp.float32)), axis=1)
    differ = (slot_real_tag[:, :, None] != slot_synth_tag[:, None, :]).astype(jnp.float32)
    return 0.5 * real_sq[:, :, None] + 0.5 * synth_sq[:, None, :] - inner_prod + PENALTY * differ


def lse_parts(scores, axis):
    highest = jnp.max(scores, axis=axis)
    mass_sum = jnp.sum(jnp.exp(scores - jnp.expand_dims(highest, axis)), axis=axis)
    return (highest, mass_sum)


def make_shards(n_blk, n_sub):
    def swap(value):
        return lax.ppermute(value, "sub", [(0, 1), (1, 0)])

    def send_up(chunks):
        moved = [chunks[0]]
        for offset in range(1, n_blk):
            perm = [(index, (index + offset) % n_blk) for index in range(n_blk)]
            moved.append(lax.ppermute(chunks[offset], "blk", perm))
        return moved

    def send_down(chunks):
        moved = [chunks[0]]
        for offset in range(1, n_blk):
            perm = [(index, (index - offset) % n_blk) for index in range(n_blk)]
            moved.append(lax.ppermute(chunks[offset], "blk", perm))
        return moved

    def shards(
        real_points,
        synth_points,
        real_cluster,
        synth_cluster,
        real_weight,
        synth_weight,
        pair_block,
        pair_row,
        pair_count,
    ):
        features, point_count = real_points.shape
        blocks = point_count // BLOCK
        marginals = real_weight.shape[0]
        half = marginals // n_sub
        peer_count, capacity = pair_block.shape
        wide = n_sub * capacity
        slot_count = peer_count * wide
        my_blk = lax.axis_index("blk")
        my_sub = lax.axis_index("sub")
        own_real = real_points.reshape(features, blocks, BLOCK)
        real_tags = real_cluster.reshape(1, blocks, BLOCK).astype(jnp.bfloat16)
        own_synth = jnp.concatenate(
            [synth_points, synth_cluster.astype(jnp.bfloat16)[None, :]], axis=0
        ).reshape(features + 1, blocks, BLOCK)
        log_real = jnp.log(
            lax.dynamic_slice_in_dim(real_weight, my_sub * half, half, 0).astype(jnp.float32) + 0.5
        ).reshape(half, blocks, BLOCK)
        log_synth = jnp.log(
            lax.dynamic_slice_in_dim(synth_weight, my_sub * half, half, 0).astype(jnp.float32) + 0.5
        ).reshape(half, blocks, BLOCK)

        peers = (my_blk + jnp.arange(peer_count, dtype=jnp.int32)) % peer_count
        everything = send_down([own_synth] * peer_count)
        lists = jnp.stack([pair_block, pair_row, jnp.broadcast_to(pair_count[:, None], pair_block.shape)])
        lists = jnp.stack([lists, swap(lists)], axis=1)
        listed = lax.broadcasted_iota(jnp.int32, lists.shape[1:], 2) < lists[2]
        wanted = pick_lead(jnp.transpose(jnp.where(listed, lists[0], 0), (1, 0, 2)), peers)
        rows_used = pick_lead(jnp.transpose(jnp.where(listed, lists[1], 0), (1, 0, 2)), peers)
        usable = pick_lead(jnp.transpose(listed.astype(jnp.int32), (1, 0, 2)), peers)
        wanted = wanted.reshape(peer_count, wide)
        rows_used = rows_used.reshape(slot_count)
        usable = usable.reshape(slot_count)[:, None, None] > 0
        far = pick_rows(
            jnp.concatenate(everything, axis=1),
            (wanted + blocks * jnp.arange(peer_count, dtype=jnp.int32)[:, None]).reshape(slot_count),
            peer_count * blocks,
        )
        far_y = far[:, :features]
        far_tags = far[:, features]
        slot_x = pick_rows(own_real, rows_used, blocks)
        slot_tags = pick_rows(real_tags, rows_used, blocks)[:, 0]
        cost_cols = slot_costs(slot_x, slot_tags, far_y, far_tags) / SMOOTH
        cost_rows = slot_costs(far_y, far_tags, slot_x, slot_tags) / SMOOTH

        def both_halves(mine):
            other = swap(mine)
            first = jnp.where(my_sub == 0, mine, other)
            second = jnp.where(my_sub == 0, other, mine)
            return jnp.concatenate([first, second], axis=0).reshape(marginals, point_count)

        synth_pot = jnp.zeros((half, blocks, BLOCK), jnp.float32)
        real_pot = jnp.zeros((half, blocks, BLOCK), jnp.float32)
        for sweep_index in range(ITERS):
            if sweep_index == 0:
                panel = jnp.zeros((slot_count, 1, BLOCK), jnp.float32)
            else:
                panel = jnp.concatenate(
                    send_down(
                        [
                            pick_rows(synth_pot, requested[offset * wide : (offset + 1) * wide], blocks)
                            for offset in range(peer_count)
                        ]
                    ),
                    axis=0,
                )
            highest, mass_sum = [], []
            for offset in range(peer_count):
                piece = slice(offset * wide, (offset + 1) * wide)
                scores = (panel[piece] / SMOOTH)[:, :, :, None] - cost_rows[piece, None]
                parts = lse_parts(scores, 2)
                highest.append(parts[0])
                mass_sum.append(parts[1])
            highest = jnp.concatenate(highest, axis=0)
            mass_sum = jnp.concatenate(mass_sum, axis=0)
            highest = jnp.where(usable, highest, SENTINEL)
            mass_sum = jnp.where(usable, mass_sum, 0.0)
            block_top, summed = fold_blocks(highest, mass_sum, rows_used, blocks)
            real_pot = finish(log_real, block_top, summed)

            own_rows = pick_rows(real_pot, rows_used, blocks)
            chunks = [None] * peer_count
            for offset in list(range(1, peer_count)) + [0]:
                piece = slice(offset * wide, (offset + 1) * wide)
                rows_here = own_rows[piece]
                if sweep_index == ITERS - 1 and offset == 0:
                    real_out, rows_here = lax.optimization_barrier((both_halves(real_pot), rows_here))
                scores = (rows_here / SMOOTH)[:, :, :, None] - cost_cols[piece, None]
                highest, mass_sum = lse_parts(scores, 2)
                lse = jnp.where(usable[piece], highest + jnp.log(mass_sum), SENTINEL)
                if sweep_index == 0:
                    block_ids = jnp.broadcast_to(
                        wanted[offset].reshape(wide, 1, 1).astype(jnp.float32), (wide, 1, BLOCK)
                    )
                    lse = jnp.concatenate([lse, block_ids], axis=1)
                chunks[offset] = lse
            back = jnp.concatenate(send_up(chunks), axis=0)
            if sweep_index == 0:
                requested = back[:, half, 0].astype(jnp.int32)
                back = back[:, :half]
            block_top, summed = fold_lse(back, requested, blocks)
            synth_pot = finish(log_synth, block_top, summed)

        return (real_out, both_halves(synth_pot))

    return shards


def solution(mesh):
    placed = (
        P(None, ("slab", "blk")),
        P(None, ("slab", "blk")),
        P(("slab", "blk")),
        P(("slab", "blk")),
        P("bag", ("slab", "blk")),
        P("bag", ("slab", "blk")),
        P(("slab", "blk", "sub"), None),
        P(("slab", "blk", "sub"), None),
        P(("slab", "blk", "sub")),
    )
    return jax.shard_map(
        make_shards(mesh.shape["blk"], mesh.shape["sub"]),
        mesh=mesh,
        in_specs=placed,
        out_specs=(P("bag", ("slab", "blk")), P("bag", ("slab", "blk"))),
        check_vma=False,
    )
```

```python
import jax
import jax.numpy as jnp
from jax import lax
from jax.sharding import PartitionSpec as P

BLOCK = 128
ITERS = 2


SMOOTH = 0.1
PENALTY = 0.3
SENTINEL = -1e30


def join_parts(earlier, latter):
    larger = jnp.maximum(earlier[0], latter[0])
    return (
        larger,
        earlier[1] * jnp.exp(earlier[0] - larger) + latter[1] * jnp.exp(latter[0] - larger),
    )


def pick_rows(values, ids, blocks):
    hits = ids[:, None] == jnp.arange(blocks, dtype=jnp.int32)[None, :]
    chosen = jnp.where(hits[:, None, :, None], values[None], jnp.zeros((), values.dtype))
    return jnp.sum(chosen, axis=2, dtype=values.dtype)


def pick_lead(values, ids):
    hits = ids[:, None] == jnp.arange(values.shape[0], dtype=jnp.int32)[None, :]
    hits = hits.reshape(hits.shape + (1,) * (values.ndim - 1))
    return jnp.sum(jnp.where(hits, values[None], jnp.zeros((), values.dtype)), axis=1, dtype=values.dtype)


def fold_blocks(highest, mass_sum, owners, blocks):
    matches = owners[:, None] == jnp.arange(blocks, dtype=jnp.int32)[None, :]
    match_mask = matches[:, None, :, None]
    block_top = jnp.max(jnp.where(match_mask, highest[:, :, None, :], SENTINEL), axis=0)
    slot_top = pick_rows(block_top, owners, blocks)
    scaled = mass_sum * jnp.exp(highest - slot_top)
    summed = jnp.sum(jnp.where(match_mask, scaled[:, :, None, :], 0.0), axis=0)
    return (block_top, summed)


def fold_lse(lse, owners, blocks):
    matches = owners[:, None] == jnp.arange(blocks, dtype=jnp.int32)[None, :]
    match_mask = matches[:, None, :, None]
    block_top = jnp.max(jnp.where(match_mask, lse[:, :, None, :], SENTINEL), axis=0)
    slot_top = pick_rows(block_top, owners, blocks)
    scaled = jnp.where(lse > 0.5 * SENTINEL, jnp.exp(lse - slot_top), 0.0)
    summed = jnp.sum(jnp.where(match_mask, scaled[:, :, None, :], 0.0), axis=0)
    return (block_top, summed)


def finish(log_weight, block_top, summed):
    spread = jnp.where(summed > 0.5, block_top + jnp.log(jnp.maximum(summed, 0.5)), 0.0)
    return SMOOTH * log_weight - SMOOTH * spread


def slot_costs(slot_real, slot_real_tag, slot_synth, slot_synth_tag):
    inner_prod = jnp.einsum(
        "gdi,gdj->gij", slot_real, slot_synth, preferred_element_type=jnp.float32
    )
    real_sq = jnp.sum(jnp.square(slot_real.astype(jnp.float32)), axis=1)
    synth_sq = jnp.sum(jnp.square(slot_synth.astype(jnp.float32)), axis=1)
    differ = (slot_real_tag[:, :, None] != slot_synth_tag[:, None, :]).astype(jnp.float32)
    return 0.5 * real_sq[:, :, None] + 0.5 * synth_sq[:, None, :] - inner_prod + PENALTY * differ


def lse_parts(scores, axis):
    highest = jnp.max(scores, axis=axis)
    mass_sum = jnp.sum(jnp.exp(scores - jnp.expand_dims(highest, axis)), axis=axis)
    return (highest, mass_sum)


def make_shards(n_blk, n_sub):
    def swap(value):
        return lax.ppermute(value, "sub", [(0, 1), (1, 0)])

    def partner(index, offset):
        if n_blk & (n_blk - 1) == 0:
            return index ^ offset
        return (index + offset) % n_blk

    def exchange(chunks, upward):
        moved = [chunks[0]]
        for offset in range(1, n_blk):
            if upward:
                perm = [(index, partner(index, offset)) for index in range(n_blk)]
            else:
                perm = [(partner(index, offset), index) for index in range(n_blk)]
            moved.append(lax.ppermute(chunks[offset], "blk", perm))
        return moved

    def send_up(chunks):
        return exchange(chunks, True)

    def send_down(chunks):
        return exchange(chunks, False)

    def shards(
        real_points,
        synth_points,
        real_cluster,
        synth_cluster,
        real_weight,
        synth_weight,
        pair_block,
        pair_row,
        pair_count,
    ):
        features, point_count = real_points.shape
        blocks = point_count // BLOCK
        marginals = real_weight.shape[0]
        half = marginals // n_sub
        peer_count, capacity = pair_block.shape
        wide = n_sub * capacity
        slot_count = peer_count * wide
        my_blk = lax.axis_index("blk")
        my_sub = lax.axis_index("sub")
        own_real = real_points.reshape(features, blocks, BLOCK)
        real_tags = real_cluster.reshape(1, blocks, BLOCK).astype(jnp.bfloat16)
        own_synth = jnp.concatenate(
            [synth_points, synth_cluster.astype(jnp.bfloat16)[None, :]], axis=0
        ).reshape(features + 1, blocks, BLOCK)
        log_real = jnp.log(
            lax.dynamic_slice_in_dim(real_weight, my_sub * half, half, 0).astype(jnp.float32) + 0.5
        ).reshape(half, blocks, BLOCK)
        log_synth = jnp.log(
            lax.dynamic_slice_in_dim(synth_weight, my_sub * half, half, 0).astype(jnp.float32) + 0.5
        ).reshape(half, blocks, BLOCK)

        offsets = jnp.arange(peer_count, dtype=jnp.int32)
        if peer_count & (peer_count - 1) == 0:
            peers = jnp.bitwise_xor(my_blk, offsets)
        else:
            peers = (my_blk + offsets) % peer_count
        everything = send_down([own_synth] * peer_count)
        lists = jnp.stack([pair_block, pair_row, jnp.broadcast_to(pair_count[:, None], pair_block.shape)])
        lists = jnp.stack([lists, swap(lists)], axis=1)
        listed = lax.broadcasted_iota(jnp.int32, lists.shape[1:], 2) < lists[2]
        wanted = pick_lead(jnp.transpose(jnp.where(listed, lists[0], 0), (1, 0, 2)), peers)
        rows_used = pick_lead(jnp.transpose(jnp.where(listed, lists[1], 0), (1, 0, 2)), peers)
        usable = pick_lead(jnp.transpose(listed.astype(jnp.int32), (1, 0, 2)), peers)
        wanted = wanted.reshape(peer_count, wide)
        rows_used = rows_used.reshape(slot_count)
        usable = usable.reshape(slot_count)[:, None, None] > 0
        far = jnp.concatenate(
            [pick_rows(everything[offset], wanted[offset], blocks) for offset in range(peer_count)], axis=0
        )
        far_y = far[:, :features]
        far_tags = far[:, features]
        slot_x = pick_rows(own_real, rows_used, blocks)
        slot_tags = pick_rows(real_tags, rows_used, blocks)[:, 0]
        cost_cols = slot_costs(slot_x, slot_tags, far_y, far_tags) / SMOOTH
        cost_rows = slot_costs(far_y, far_tags, slot_x, slot_tags) / SMOOTH

        synth_pot = jnp.zeros((half, blocks, BLOCK), jnp.float32)
        real_pot = jnp.zeros((half, blocks, BLOCK), jnp.float32)
        for sweep_index in range(ITERS):
            if sweep_index == 0:
                panel = jnp.zeros((slot_count, 1, BLOCK), jnp.float32)
            else:
                panel = jnp.concatenate(
                    send_down(
                        [
                            pick_rows(synth_pot, requested[offset * wide : (offset + 1) * wide], blocks)
                            for offset in range(peer_count)
                        ]
                    ),
                    axis=0,
                )
            highest, mass_sum = [], []
            for offset in range(peer_count):
                piece = slice(offset * wide, (offset + 1) * wide)
                scores = (panel[piece] / SMOOTH)[:, :, :, None] - cost_rows[piece, None]
                parts = lse_parts(scores, 2)
                highest.append(parts[0])
                mass_sum.append(parts[1])
            highest = jnp.concatenate(highest, axis=0)
            mass_sum = jnp.concatenate(mass_sum, axis=0)
            highest = jnp.where(usable, highest, SENTINEL)
            mass_sum = jnp.where(usable, mass_sum, 0.0)
            block_top, summed = fold_blocks(highest, mass_sum, rows_used, blocks)
            real_pot = finish(log_real, block_top, summed)

            own_rows = pick_rows(real_pot, rows_used, blocks)
            chunks = [None] * peer_count
            for offset in list(range(1, peer_count)) + [0]:
                piece = slice(offset * wide, (offset + 1) * wide)
                scores = (own_rows[piece] / SMOOTH)[:, :, :, None] - cost_cols[piece, None]
                highest, mass_sum = lse_parts(scores, 2)
                lse = jnp.where(usable[piece], highest + jnp.log(mass_sum), SENTINEL)
                if sweep_index == 0:
                    block_ids = jnp.broadcast_to(
                        wanted[offset].reshape(wide, 1, 1).astype(jnp.float32), (wide, 1, BLOCK)
                    )
                    lse = jnp.concatenate([lse, block_ids], axis=1)
                chunks[offset] = lse
            back = jnp.concatenate(send_up(chunks), axis=0)
            if sweep_index == 0:
                requested = back[:, half, 0].astype(jnp.int32)
                back = back[:, :half]
            block_top, summed = fold_lse(back, requested, blocks)
            synth_pot = finish(log_synth, block_top, summed)

        def both_halves(mine):
            other = swap(mine)
            first = jnp.where(my_sub == 0, mine, other)
            second = jnp.where(my_sub == 0, other, mine)
            return jnp.concatenate([first, second], axis=0).reshape(marginals, point_count)

        return (both_halves(real_pot), both_halves(synth_pot))

    return shards


def solution(mesh):
    placed = (
        P(None, ("slab", "blk")),
        P(None, ("slab", "blk")),
        P(("slab", "blk")),
        P(("slab", "blk")),
        P("bag", ("slab", "blk")),
        P("bag", ("slab", "blk")),
        P(("slab", "blk", "sub"), None),
        P(("slab", "blk", "sub"), None),
        P(("slab", "blk", "sub")),
    )
    return jax.shard_map(
        make_shards(mesh.shape["blk"], mesh.shape["sub"]),
        mesh=mesh,
        in_specs=placed,
        out_specs=(P("bag", ("slab", "blk")), P("bag", ("slab", "blk"))),
        check_vma=False,
    )
```

```python
import jax
import jax.numpy as jnp
from jax import lax
from jax.sharding import PartitionSpec as P

BLOCK = 128
ITERS = 2


SMOOTH = 0.1
PENALTY = 0.3
SENTINEL = -1e30


def join_parts(earlier, latter):
    larger = jnp.maximum(earlier[0], latter[0])
    return (
        larger,
        earlier[1] * jnp.exp(earlier[0] - larger) + latter[1] * jnp.exp(latter[0] - larger),
    )


def pick_rows(values, ids, blocks):
    hits = ids[:, None] == jnp.arange(blocks, dtype=jnp.int32)[None, :]
    chosen = jnp.where(hits[:, None, :, None], values[None], jnp.zeros((), values.dtype))
    return jnp.sum(chosen, axis=2, dtype=values.dtype)


def pick_lead(values, ids):
    hits = ids[:, None] == jnp.arange(values.shape[0], dtype=jnp.int32)[None, :]
    hits = hits.reshape(hits.shape + (1,) * (values.ndim - 1))
    return jnp.sum(jnp.where(hits, values[None], jnp.zeros((), values.dtype)), axis=1, dtype=values.dtype)


def fold_blocks(highest, mass_sum, owners, blocks):
    matches = owners[:, None] == jnp.arange(blocks, dtype=jnp.int32)[None, :]
    match_mask = matches[:, None, :, None]
    block_top = jnp.max(jnp.where(match_mask, highest[:, :, None, :], SENTINEL), axis=0)
    slot_top = pick_rows(block_top, owners, blocks)
    scaled = mass_sum * jnp.exp(highest - slot_top)
    summed = jnp.sum(jnp.where(match_mask, scaled[:, :, None, :], 0.0), axis=0)
    return (block_top, summed)


def fold_lse(lse, owners, blocks):
    matches = owners[:, None] == jnp.arange(blocks, dtype=jnp.int32)[None, :]
    match_mask = matches[:, None, :, None]
    block_top = jnp.max(jnp.where(match_mask, lse[:, :, None, :], SENTINEL), axis=0)
    slot_top = pick_rows(block_top, owners, blocks)
    scaled = jnp.where(lse > 0.5 * SENTINEL, jnp.exp(lse - slot_top), 0.0)
    summed = jnp.sum(jnp.where(match_mask, scaled[:, :, None, :], 0.0), axis=0)
    return (block_top, summed)


def finish(log_weight, block_top, summed):
    spread = jnp.where(summed > 0.5, block_top + jnp.log(jnp.maximum(summed, 0.5)), 0.0)
    return SMOOTH * log_weight - SMOOTH * spread


def slot_costs(slot_real, slot_real_tag, slot_synth, slot_synth_tag):
    inner_prod = jnp.einsum(
        "gdi,gdj->gij", slot_real, slot_synth, preferred_element_type=jnp.float32
    )
    real_sq = jnp.sum(jnp.square(slot_real.astype(jnp.float32)), axis=1)
    synth_sq = jnp.sum(jnp.square(slot_synth.astype(jnp.float32)), axis=1)
    differ = (slot_real_tag[:, :, None] != slot_synth_tag[:, None, :]).astype(jnp.float32)
    return 0.5 * real_sq[:, :, None] + 0.5 * synth_sq[:, None, :] - inner_prod + PENALTY * differ


def lse_parts(scores, axis):
    highest = jnp.max(scores, axis=axis)
    mass_sum = jnp.sum(jnp.exp(scores - jnp.expand_dims(highest, axis)), axis=axis)
    return (highest, mass_sum)


def make_shards(n_blk, n_sub):
    def swap(value):
        return lax.ppermute(value, "sub", [(0, 1), (1, 0)])

    def partner(index, offset):
        if n_blk & (n_blk - 1) == 0:
            return index ^ offset
        return (index + offset) % n_blk

    def exchange(chunks, upward):
        moved = [chunks[0]]
        for offset in range(1, n_blk):
            if upward:
                perm = [(index, partner(index, offset)) for index in range(n_blk)]
            else:
                perm = [(partner(index, offset), index) for index in range(n_blk)]
            moved.append(lax.ppermute(chunks[offset], "blk", perm))
        return moved

    def send_up(chunks):
        return exchange(chunks, True)

    def send_down(chunks):
        return exchange(chunks, False)

    def shards(
        real_points,
        synth_points,
        real_cluster,
        synth_cluster,
        real_weight,
        synth_weight,
        pair_block,
        pair_row,
        pair_count,
    ):
        features, point_count = real_points.shape
        blocks = point_count // BLOCK
        marginals = real_weight.shape[0]
        half = marginals // n_sub
        peer_count, capacity = pair_block.shape
        wide = n_sub * capacity
        slot_count = peer_count * wide
        my_blk = lax.axis_index("blk")
        my_sub = lax.axis_index("sub")
        own_real = real_points.reshape(features, blocks, BLOCK)
        real_tags = real_cluster.reshape(1, blocks, BLOCK).astype(jnp.bfloat16)
        own_synth = jnp.concatenate(
            [synth_points, synth_cluster.astype(jnp.bfloat16)[None, :]], axis=0
        ).reshape(features + 1, blocks, BLOCK)
        log_real = jnp.log(
            lax.dynamic_slice_in_dim(real_weight, my_sub * half, half, 0).astype(jnp.float32) + 0.5
        ).reshape(half, blocks, BLOCK)
        log_synth = jnp.log(
            lax.dynamic_slice_in_dim(synth_weight, my_sub * half, half, 0).astype(jnp.float32) + 0.5
        ).reshape(half, blocks, BLOCK)

        offsets = jnp.arange(peer_count, dtype=jnp.int32)
        if peer_count & (peer_count - 1) == 0:
            peers = jnp.bitwise_xor(my_blk, offsets)
        else:
            peers = (my_blk + offsets) % peer_count
        everything = send_down([own_synth] * peer_count)
        lists = jnp.stack([pair_block, pair_row, jnp.broadcast_to(pair_count[:, None], pair_block.shape)])
        lists = jnp.stack([lists, swap(lists)], axis=1)
        listed = lax.broadcasted_iota(jnp.int32, lists.shape[1:], 2) < lists[2]
        wanted = pick_lead(jnp.transpose(jnp.where(listed, lists[0], 0), (1, 0, 2)), peers)
        rows_used = pick_lead(jnp.transpose(jnp.where(listed, lists[1], 0), (1, 0, 2)), peers)
        usable = pick_lead(jnp.transpose(listed.astype(jnp.int32), (1, 0, 2)), peers)
        wanted = wanted.reshape(peer_count, wide)
        rows_used = rows_used.reshape(slot_count)
        usable = usable.reshape(slot_count)[:, None, None] > 0
        cost_cols, cost_rows = [], []
        for offset in range(peer_count):
            piece = slice(offset * wide, (offset + 1) * wide)
            far = pick_rows(everything[offset], wanted[offset], blocks)
            far_y = far[:, :features]
            far_tags = far[:, features]
            slot_x = pick_rows(own_real, rows_used[piece], blocks)
            slot_tags = pick_rows(real_tags, rows_used[piece], blocks)[:, 0]
            cost_cols.append(slot_costs(slot_x, slot_tags, far_y, far_tags) / SMOOTH)
            cost_rows.append(slot_costs(far_y, far_tags, slot_x, slot_tags) / SMOOTH)

        synth_pot = jnp.zeros((half, blocks, BLOCK), jnp.float32)
        real_pot = jnp.zeros((half, blocks, BLOCK), jnp.float32)
        for sweep_index in range(ITERS):
            if sweep_index == 0:
                panel = jnp.zeros((slot_count, 1, BLOCK), jnp.float32)
            else:
                panel = jnp.concatenate(
                    send_down(
                        [
                            pick_rows(synth_pot, requested[offset * wide : (offset + 1) * wide], blocks)
                            for offset in range(peer_count)
                        ]
                    ),
                    axis=0,
                )
            highest, mass_sum = [], []
            for offset in range(peer_count):
                piece = slice(offset * wide, (offset + 1) * wide)
                scores = (panel[piece] / SMOOTH)[:, :, :, None] - cost_rows[offset][:, None]
                parts = lse_parts(scores, 2)
                highest.append(parts[0])
                mass_sum.append(parts[1])
            highest = jnp.concatenate(highest, axis=0)
            mass_sum = jnp.concatenate(mass_sum, axis=0)
            highest = jnp.where(usable, highest, SENTINEL)
            mass_sum = jnp.where(usable, mass_sum, 0.0)
            block_top, summed = fold_blocks(highest, mass_sum, rows_used, blocks)
            real_pot = finish(log_real, block_top, summed)

            own_rows = pick_rows(real_pot, rows_used, blocks)
            chunks = [None] * peer_count
            for offset in list(range(1, peer_count)) + [0]:
                piece = slice(offset * wide, (offset + 1) * wide)
                scores = (own_rows[piece] / SMOOTH)[:, :, :, None] - cost_cols[offset][:, None]
                highest, mass_sum = lse_parts(scores, 2)
                lse = jnp.where(usable[piece], highest + jnp.log(mass_sum), SENTINEL)
                if sweep_index == 0:
                    block_ids = jnp.broadcast_to(
                        wanted[offset].reshape(wide, 1, 1).astype(jnp.float32), (wide, 1, BLOCK)
                    )
                    lse = jnp.concatenate([lse, block_ids], axis=1)
                chunks[offset] = lse
            back = jnp.concatenate(send_up(chunks), axis=0)
            if sweep_index == 0:
                requested = back[:, half, 0].astype(jnp.int32)
                back = back[:, :half]
            block_top, summed = fold_lse(back, requested, blocks)
            synth_pot = finish(log_synth, block_top, summed)

        def both_halves(mine):
            other = swap(mine)
            first = jnp.where(my_sub == 0, mine, other)
            second = jnp.where(my_sub == 0, other, mine)
            return jnp.concatenate([first, second], axis=0).reshape(marginals, point_count)

        return (both_halves(real_pot), both_halves(synth_pot))

    return shards


def solution(mesh):
    placed = (
        P(None, ("slab", "blk")),
        P(None, ("slab", "blk")),
        P(("slab", "blk")),
        P(("slab", "blk")),
        P("bag", ("slab", "blk")),
        P("bag", ("slab", "blk")),
        P(("slab", "blk", "sub"), None),
        P(("slab", "blk", "sub"), None),
        P(("slab", "blk", "sub")),
    )
    return jax.shard_map(
        make_shards(mesh.shape["blk"], mesh.shape["sub"]),
        mesh=mesh,
        in_specs=placed,
        out_specs=(P("bag", ("slab", "blk")), P("bag", ("slab", "blk"))),
        check_vma=False,
    )
```

```python
import jax
import jax.numpy as jnp
from jax import lax
from jax.sharding import PartitionSpec as P

BLOCK = 128
ITERS = 2


SMOOTH = 0.1
PENALTY = 0.3
SENTINEL = -1e30


def join_parts(earlier, latter):
    larger = jnp.maximum(earlier[0], latter[0])
    return (
        larger,
        earlier[1] * jnp.exp(earlier[0] - larger) + latter[1] * jnp.exp(latter[0] - larger),
    )


def pick_rows(values, ids, blocks):
    hits = ids[:, None] == jnp.arange(blocks, dtype=jnp.int32)[None, :]
    chosen = jnp.where(hits[:, None, :, None], values[None], jnp.zeros((), values.dtype))
    return jnp.sum(chosen, axis=2, dtype=values.dtype)


def pick_lead(values, ids):
    hits = ids[:, None] == jnp.arange(values.shape[0], dtype=jnp.int32)[None, :]
    hits = hits.reshape(hits.shape + (1,) * (values.ndim - 1))
    return jnp.sum(jnp.where(hits, values[None], jnp.zeros((), values.dtype)), axis=1, dtype=values.dtype)


def fold_blocks(highest, mass_sum, owners, blocks):
    matches = owners[:, None] == jnp.arange(blocks, dtype=jnp.int32)[None, :]
    match_mask = matches[:, None, :, None]
    block_top = jnp.max(jnp.where(match_mask, highest[:, :, None, :], SENTINEL), axis=0)
    slot_top = pick_rows(block_top, owners, blocks)
    scaled = mass_sum * jnp.exp(highest - slot_top)
    summed = jnp.sum(jnp.where(match_mask, scaled[:, :, None, :], 0.0), axis=0)
    return (block_top, summed)


def fold_lse(lse, owners, blocks):
    matches = owners[:, None] == jnp.arange(blocks, dtype=jnp.int32)[None, :]
    match_mask = matches[:, None, :, None]
    block_top = jnp.max(jnp.where(match_mask, lse[:, :, None, :], SENTINEL), axis=0)
    slot_top = pick_rows(block_top, owners, blocks)
    scaled = jnp.where(lse > 0.5 * SENTINEL, jnp.exp(lse - slot_top), 0.0)
    summed = jnp.sum(jnp.where(match_mask, scaled[:, :, None, :], 0.0), axis=0)
    return (block_top, summed)


def finish(log_weight, block_top, summed):
    spread = jnp.where(summed > 0.5, block_top + jnp.log(jnp.maximum(summed, 0.5)), 0.0)
    return SMOOTH * log_weight - SMOOTH * spread


def slot_costs(slot_real, slot_real_tag, slot_synth, slot_synth_tag):
    inner_prod = jnp.einsum(
        "gdi,gdj->gij", slot_real, slot_synth, preferred_element_type=jnp.float32
    )
    real_sq = jnp.sum(jnp.square(slot_real.astype(jnp.float32)), axis=1)
    synth_sq = jnp.sum(jnp.square(slot_synth.astype(jnp.float32)), axis=1)
    differ = (slot_real_tag[:, :, None] != slot_synth_tag[:, None, :]).astype(jnp.float32)
    return 0.5 * real_sq[:, :, None] + 0.5 * synth_sq[:, None, :] - inner_prod + PENALTY * differ


def lse_parts(scores, axis):
    highest = jnp.max(scores, axis=axis)
    mass_sum = jnp.sum(jnp.exp(scores - jnp.expand_dims(highest, axis)), axis=axis)
    return (highest, mass_sum)


def make_shards(n_blk, n_sub):
    def swap(value):
        return lax.ppermute(value, "sub", [(0, 1), (1, 0)])

    def partner(index, offset):
        if n_blk & (n_blk - 1) == 0:
            return index ^ offset
        return (index + offset) % n_blk

    def exchange(chunks, upward):
        moved = [chunks[0]]
        for offset in range(1, n_blk):
            if upward:
                perm = [(index, partner(index, offset)) for index in range(n_blk)]
            else:
                perm = [(partner(index, offset), index) for index in range(n_blk)]
            moved.append(lax.ppermute(chunks[offset], "blk", perm))
        return moved

    def send_up(chunks):
        return exchange(chunks, True)

    def send_down(chunks):
        return exchange(chunks, False)

    def shards(
        real_points,
        synth_points,
        real_cluster,
        synth_cluster,
        real_weight,
        synth_weight,
        pair_block,
        pair_row,
        pair_count,
    ):
        features, point_count = real_points.shape
        blocks = point_count // BLOCK
        marginals = real_weight.shape[0]
        half = marginals // n_sub
        peer_count, capacity = pair_block.shape
        wide = n_sub * capacity
        slot_count = peer_count * wide
        my_blk = lax.axis_index("blk")
        my_sub = lax.axis_index("sub")
        own_real = real_points.reshape(features, blocks, BLOCK)
        real_tags = real_cluster.reshape(1, blocks, BLOCK).astype(jnp.bfloat16)
        own_synth = jnp.concatenate([synth_points, synth_cluster.astype(jnp.bfloat16)[None, :]], axis=0)
        log_real_flat = jnp.log(
            lax.dynamic_slice_in_dim(real_weight, my_sub * half, half, 0).astype(jnp.float32) + 0.5
        )
        log_synth_flat = jnp.log(
            lax.dynamic_slice_in_dim(synth_weight, my_sub * half, half, 0).astype(jnp.float32) + 0.5
        )
        log_real = log_real_flat.reshape(half, blocks, BLOCK)
        log_synth = log_synth_flat.reshape(half, blocks, BLOCK)

        offsets = jnp.arange(peer_count, dtype=jnp.int32)
        if peer_count & (peer_count - 1) == 0:
            peers = jnp.bitwise_xor(my_blk, offsets)
        else:
            peers = (my_blk + offsets) % peer_count
        everything = send_down([own_synth] * peer_count)
        lists = jnp.stack([pair_block, pair_row, jnp.broadcast_to(pair_count[:, None], pair_block.shape)])
        lists = jnp.stack([lists, swap(lists)], axis=1)
        listed = lax.broadcasted_iota(jnp.int32, lists.shape[1:], 2) < lists[2]
        wanted = pick_lead(jnp.transpose(jnp.where(listed, lists[0], 0), (1, 0, 2)), peers)
        rows_used = pick_lead(jnp.transpose(jnp.where(listed, lists[1], 0), (1, 0, 2)), peers)
        usable = pick_lead(jnp.transpose(listed.astype(jnp.int32), (1, 0, 2)), peers)
        wanted = wanted.reshape(peer_count, wide)
        rows_used = rows_used.reshape(slot_count)
        usable = usable.reshape(slot_count)[:, None, None] > 0
        far = jnp.concatenate(
            [
                pick_rows(everything[offset].reshape(features + 1, blocks, BLOCK), wanted[offset], blocks)
                for offset in range(peer_count)
            ],
            axis=0,
        )
        far_y = far[:, :features]
        far_tags = far[:, features]
        slot_x = pick_rows(own_real, rows_used, blocks)
        slot_tags = pick_rows(real_tags, rows_used, blocks)[:, 0]
        cost_cols = slot_costs(slot_x, slot_tags, far_y, far_tags) / SMOOTH
        cost_rows = slot_costs(far_y, far_tags, slot_x, slot_tags) / SMOOTH

        synth_pot = jnp.zeros((half, blocks, BLOCK), jnp.float32)
        real_pot = jnp.zeros((half, blocks, BLOCK), jnp.float32)
        for sweep_index in range(ITERS):
            if sweep_index == 0:
                panel = jnp.zeros((slot_count, 1, BLOCK), jnp.float32)
            else:
                panel = jnp.concatenate(
                    send_down(
                        [
                            pick_rows(synth_pot, requested[offset * wide : (offset + 1) * wide], blocks)
                            for offset in range(peer_count)
                        ]
                    ),
                    axis=0,
                )
            highest, mass_sum = [], []
            for offset in range(peer_count):
                piece = slice(offset * wide, (offset + 1) * wide)
                scores = (panel[piece] / SMOOTH)[:, :, :, None] - cost_rows[piece, None]
                parts = lse_parts(scores, 2)
                highest.append(parts[0])
                mass_sum.append(parts[1])
            highest = jnp.concatenate(highest, axis=0)
            mass_sum = jnp.concatenate(mass_sum, axis=0)
            highest = jnp.where(usable, highest, SENTINEL)
            mass_sum = jnp.where(usable, mass_sum, 0.0)
            block_top, summed = fold_blocks(highest, mass_sum, rows_used, blocks)
            if sweep_index == ITERS - 1:
                real_flat = finish(
                    log_real_flat, block_top.reshape(half, point_count), summed.reshape(half, point_count)
                )
                real_pot = real_flat.reshape(half, blocks, BLOCK)
            else:
                real_pot = finish(log_real, block_top, summed)

            own_rows = pick_rows(real_pot, rows_used, blocks)
            chunks = [None] * peer_count
            for offset in list(range(1, peer_count)) + [0]:
                piece = slice(offset * wide, (offset + 1) * wide)
                scores = (own_rows[piece] / SMOOTH)[:, :, :, None] - cost_cols[piece, None]
                highest, mass_sum = lse_parts(scores, 2)
                lse = jnp.where(usable[piece], highest + jnp.log(mass_sum), SENTINEL)
                if sweep_index == 0:
                    block_ids = jnp.broadcast_to(
                        wanted[offset].reshape(wide, 1, 1).astype(jnp.float32), (wide, 1, BLOCK)
                    )
                    lse = jnp.concatenate([lse, block_ids], axis=1)
                chunks[offset] = lse
            back = jnp.concatenate(send_up(chunks), axis=0)
            if sweep_index == 0:
                requested = back[:, half, 0].astype(jnp.int32)
                back = back[:, :half]
            block_top, summed = fold_lse(back, requested, blocks)
            if sweep_index == ITERS - 1:
                synth_flat = finish(
                    log_synth_flat, block_top.reshape(half, point_count), summed.reshape(half, point_count)
                )
            else:
                synth_pot = finish(log_synth, block_top, summed)

        def both_halves(mine):
            other = swap(mine)
            first = jnp.where(my_sub == 0, mine, other)
            second = jnp.where(my_sub == 0, other, mine)
            return jnp.concatenate([first, second], axis=0)

        return (both_halves(real_flat), both_halves(synth_flat))

    return shards


def solution(mesh):
    placed = (
        P(None, ("slab", "blk")),
        P(None, ("slab", "blk")),
        P(("slab", "blk")),
        P(("slab", "blk")),
        P("bag", ("slab", "blk")),
        P("bag", ("slab", "blk")),
        P(("slab", "blk", "sub"), None),
        P(("slab", "blk", "sub"), None),
        P(("slab", "blk", "sub")),
    )
    return jax.shard_map(
        make_shards(mesh.shape["blk"], mesh.shape["sub"]),
        mesh=mesh,
        in_specs=placed,
        out_specs=(P("bag", ("slab", "blk")), P("bag", ("slab", "blk"))),
        check_vma=False,
    )
```

```python
import jax
import jax.numpy as jnp
from jax import lax
from jax.sharding import PartitionSpec as P

BLOCK = 128
ITERS = 2


SMOOTH = 0.1
PENALTY = 0.3
SENTINEL = -1e30


def join_parts(earlier, latter):
    larger = jnp.maximum(earlier[0], latter[0])
    return (
        larger,
        earlier[1] * jnp.exp(earlier[0] - larger) + latter[1] * jnp.exp(latter[0] - larger),
    )


def pick_rows(values, ids, blocks):
    hits = ids[:, None] == jnp.arange(blocks, dtype=jnp.int32)[None, :]
    chosen = jnp.where(hits[:, None, :, None], values[None], jnp.zeros((), values.dtype))
    return jnp.sum(chosen, axis=2, dtype=values.dtype)


def pick_lead(values, ids):
    hits = ids[:, None] == jnp.arange(values.shape[0], dtype=jnp.int32)[None, :]
    hits = hits.reshape(hits.shape + (1,) * (values.ndim - 1))
    return jnp.sum(jnp.where(hits, values[None], jnp.zeros((), values.dtype)), axis=1, dtype=values.dtype)


def fold_blocks(highest, mass_sum, owners, blocks):
    matches = owners[:, None] == jnp.arange(blocks, dtype=jnp.int32)[None, :]
    match_mask = matches[:, None, :, None]
    block_top = jnp.max(jnp.where(match_mask, highest[:, :, None, :], SENTINEL), axis=0)
    slot_top = pick_rows(block_top, owners, blocks)
    scaled = mass_sum * jnp.exp(highest - slot_top)
    summed = jnp.sum(jnp.where(match_mask, scaled[:, :, None, :], 0.0), axis=0)
    return (block_top, summed)


def fold_lse(lse, owners, blocks):
    matches = owners[:, None] == jnp.arange(blocks, dtype=jnp.int32)[None, :]
    match_mask = matches[:, None, :, None]
    block_top = jnp.max(jnp.where(match_mask, lse[:, :, None, :], SENTINEL), axis=0)
    slot_top = pick_rows(block_top, owners, blocks)
    scaled = jnp.where(lse > 0.5 * SENTINEL, jnp.exp(lse - slot_top), 0.0)
    summed = jnp.sum(jnp.where(match_mask, scaled[:, :, None, :], 0.0), axis=0)
    return (block_top, summed)


def finish(log_weight, block_top, summed):
    spread = jnp.where(summed > 0.5, block_top + jnp.log(jnp.maximum(summed, 0.5)), 0.0)
    return SMOOTH * log_weight - SMOOTH * spread


def slot_costs(slot_real, slot_real_tag, slot_synth, slot_synth_tag):
    inner_prod = jnp.einsum(
        "gdi,gdj->gij", slot_real, slot_synth, preferred_element_type=jnp.float32
    )
    real_sq = jnp.sum(jnp.square(slot_real.astype(jnp.float32)), axis=1)
    synth_sq = jnp.sum(jnp.square(slot_synth.astype(jnp.float32)), axis=1)
    differ = (slot_real_tag[:, :, None] != slot_synth_tag[:, None, :]).astype(jnp.float32)
    return 0.5 * real_sq[:, :, None] + 0.5 * synth_sq[:, None, :] - inner_prod + PENALTY * differ


def lse_parts(scores, axis):
    highest = jnp.max(scores, axis=axis)
    mass_sum = jnp.sum(jnp.exp(scores - jnp.expand_dims(highest, axis)), axis=axis)
    return (highest, mass_sum)


def make_shards(n_blk, n_sub):
    def swap(value):
        return lax.ppermute(value, "sub", [(0, 1), (1, 0)])

    def partner(index, offset):
        if n_blk & (n_blk - 1) == 0:
            return index ^ offset
        return (index + offset) % n_blk

    def exchange(chunks, upward):
        moved = [chunks[0]]
        for offset in range(1, n_blk):
            if upward:
                perm = [(index, partner(index, offset)) for index in range(n_blk)]
            else:
                perm = [(partner(index, offset), index) for index in range(n_blk)]
            moved.append(lax.ppermute(chunks[offset], "blk", perm))
        return moved

    def send_up(chunks):
        return exchange(chunks, True)

    def send_down(chunks):
        return exchange(chunks, False)

    def shards(
        real_points,
        synth_points,
        real_cluster,
        synth_cluster,
        real_weight,
        synth_weight,
        pair_block,
        pair_row,
        pair_count,
    ):
        features, point_count = real_points.shape
        blocks = point_count // BLOCK
        marginals = real_weight.shape[0]
        half = marginals // n_sub
        peer_count, capacity = pair_block.shape
        wide = n_sub * capacity
        slot_count = peer_count * wide
        my_blk = lax.axis_index("blk")
        my_sub = lax.axis_index("sub")
        own_real = real_points.reshape(features, blocks, BLOCK)
        real_tags = real_cluster.reshape(1, blocks, BLOCK)
        log_real = jnp.log(
            lax.dynamic_slice_in_dim(real_weight, my_sub * half, half, 0).astype(jnp.float32) + 0.5
        ).reshape(half, blocks, BLOCK)
        log_synth = jnp.log(
            lax.dynamic_slice_in_dim(synth_weight, my_sub * half, half, 0).astype(jnp.float32) + 0.5
        ).reshape(half, blocks, BLOCK)

        offsets = jnp.arange(peer_count, dtype=jnp.int32)
        if peer_count & (peer_count - 1) == 0:
            peers = jnp.bitwise_xor(my_blk, offsets)
        else:
            peers = (my_blk + offsets) % peer_count
        everything = send_down([synth_points] * peer_count)
        everything_tags = send_down([synth_cluster] * peer_count)
        lists = jnp.stack([pair_block, pair_row, jnp.broadcast_to(pair_count[:, None], pair_block.shape)])
        lists = jnp.stack([lists, swap(lists)], axis=1)
        listed = lax.broadcasted_iota(jnp.int32, lists.shape[1:], 2) < lists[2]
        wanted = pick_lead(jnp.transpose(jnp.where(listed, lists[0], 0), (1, 0, 2)), peers)
        rows_used = pick_lead(jnp.transpose(jnp.where(listed, lists[1], 0), (1, 0, 2)), peers)
        usable = pick_lead(jnp.transpose(listed.astype(jnp.int32), (1, 0, 2)), peers)
        wanted = wanted.reshape(peer_count, wide)
        rows_used = rows_used.reshape(slot_count)
        usable = usable.reshape(slot_count)[:, None, None] > 0
        far_y = jnp.concatenate(
            [
                pick_rows(everything[offset].reshape(features, blocks, BLOCK), wanted[offset], blocks)
                for offset in range(peer_count)
            ],
            axis=0,
        )
        far_tags = jnp.concatenate(
            [
                pick_rows(everything_tags[offset].reshape(1, blocks, BLOCK), wanted[offset], blocks)[:, 0]
                for offset in range(peer_count)
            ],
            axis=0,
        )
        slot_x = pick_rows(own_real, rows_used, blocks)
        slot_tags = pick_rows(real_tags, rows_used, blocks)[:, 0]
        cost_cols = slot_costs(slot_x, slot_tags, far_y, far_tags) / SMOOTH
        cost_rows = slot_costs(far_y, far_tags, slot_x, slot_tags) / SMOOTH

        synth_pot = jnp.zeros((half, blocks, BLOCK), jnp.float32)
        real_pot = jnp.zeros((half, blocks, BLOCK), jnp.float32)
        for sweep_index in range(ITERS):
            if sweep_index == 0:
                panel = jnp.zeros((slot_count, 1, BLOCK), jnp.float32)
            else:
                panel = jnp.concatenate(
                    send_down(
                        [
                            pick_rows(synth_pot, requested[offset * wide : (offset + 1) * wide], blocks)
                            for offset in range(peer_count)
                        ]
                    ),
                    axis=0,
                )
            highest, mass_sum = [], []
            for offset in range(peer_count):
                piece = slice(offset * wide, (offset + 1) * wide)
                scores = (panel[piece] / SMOOTH)[:, :, :, None] - cost_rows[piece, None]
                parts = lse_parts(scores, 2)
                highest.append(parts[0])
                mass_sum.append(parts[1])
            highest = jnp.concatenate(highest, axis=0)
            mass_sum = jnp.concatenate(mass_sum, axis=0)
            highest = jnp.where(usable, highest, SENTINEL)
            mass_sum = jnp.where(usable, mass_sum, 0.0)
            block_top, summed = fold_blocks(highest, mass_sum, rows_used, blocks)
            real_pot = finish(log_real, block_top, summed)

            own_rows = pick_rows(real_pot, rows_used, blocks)
            chunks = [None] * peer_count
            for offset in list(range(1, peer_count)) + [0]:
                piece = slice(offset * wide, (offset + 1) * wide)
                scores = (own_rows[piece] / SMOOTH)[:, :, :, None] - cost_cols[piece, None]
                highest, mass_sum = lse_parts(scores, 2)
                lse = jnp.where(usable[piece], highest + jnp.log(mass_sum), SENTINEL)
                if sweep_index == 0:
                    block_ids = jnp.broadcast_to(
                        wanted[offset].reshape(wide, 1, 1).astype(jnp.float32), (wide, 1, BLOCK)
                    )
                    lse = jnp.concatenate([lse, block_ids], axis=1)
                chunks[offset] = lse
            back = jnp.concatenate(send_up(chunks), axis=0)
            if sweep_index == 0:
                requested = back[:, half, 0].astype(jnp.int32)
                back = back[:, :half]
            block_top, summed = fold_lse(back, requested, blocks)
            synth_pot = finish(log_synth, block_top, summed)

        def both_halves(mine):
            other = swap(mine)
            first = jnp.where(my_sub == 0, mine, other)
            second = jnp.where(my_sub == 0, other, mine)
            return jnp.concatenate([first, second], axis=0).reshape(marginals, point_count)

        return (both_halves(real_pot), both_halves(synth_pot))

    return shards


def solution(mesh):
    placed = (
        P(None, ("slab", "blk")),
        P(None, ("slab", "blk")),
        P(("slab", "blk")),
        P(("slab", "blk")),
        P("bag", ("slab", "blk")),
        P("bag", ("slab", "blk")),
        P(("slab", "blk", "sub"), None),
        P(("slab", "blk", "sub"), None),
        P(("slab", "blk", "sub")),
    )
    return jax.shard_map(
        make_shards(mesh.shape["blk"], mesh.shape["sub"]),
        mesh=mesh,
        in_specs=placed,
        out_specs=(P("bag", ("slab", "blk")), P("bag", ("slab", "blk"))),
        check_vma=False,
    )
```

```python
import jax
import jax.numpy as jnp
from jax import lax
from jax.sharding import PartitionSpec as P

BLOCK = 128
ITERS = 2


SMOOTH = 0.1
PENALTY = 0.3
SENTINEL = -1e30


def join_parts(earlier, latter):
    larger = jnp.maximum(earlier[0], latter[0])
    return (
        larger,
        earlier[1] * jnp.exp(earlier[0] - larger) + latter[1] * jnp.exp(latter[0] - larger),
    )


def pick_rows(values, ids, blocks):
    hits = ids[:, None] == jnp.arange(blocks, dtype=jnp.int32)[None, :]
    chosen = jnp.where(hits[:, None, :, None], values[None], jnp.zeros((), values.dtype))
    return jnp.sum(chosen, axis=2, dtype=values.dtype)


def pick_lead(values, ids):
    hits = ids[:, None] == jnp.arange(values.shape[0], dtype=jnp.int32)[None, :]
    hits = hits.reshape(hits.shape + (1,) * (values.ndim - 1))
    return jnp.sum(jnp.where(hits, values[None], jnp.zeros((), values.dtype)), axis=1, dtype=values.dtype)


def fold_blocks(highest, mass_sum, owners, blocks):
    matches = owners[:, None] == jnp.arange(blocks, dtype=jnp.int32)[None, :]
    match_mask = matches[:, None, :, None]
    block_top = jnp.max(jnp.where(match_mask, highest[:, :, None, :], SENTINEL), axis=0)
    slot_top = pick_rows(block_top, owners, blocks)
    scaled = mass_sum * jnp.exp(highest - slot_top)
    summed = jnp.sum(jnp.where(match_mask, scaled[:, :, None, :], 0.0), axis=0)
    return (block_top, summed)


def fold_lse(lse, owners, blocks):
    matches = owners[:, None] == jnp.arange(blocks, dtype=jnp.int32)[None, :]
    match_mask = matches[:, None, :, None]
    block_top = jnp.max(jnp.where(match_mask, lse[:, :, None, :], SENTINEL), axis=0)
    slot_top = pick_rows(block_top, owners, blocks)
    scaled = jnp.where(lse > 0.5 * SENTINEL, jnp.exp(lse - slot_top), 0.0)
    summed = jnp.sum(jnp.where(match_mask, scaled[:, :, None, :], 0.0), axis=0)
    return (block_top, summed)


def finish(log_weight, block_top, summed):
    spread = jnp.where(summed > 0.5, block_top + jnp.log(jnp.maximum(summed, 0.5)), 0.0)
    return SMOOTH * log_weight - SMOOTH * spread


def slot_costs(slot_real, slot_real_tag, slot_synth, slot_synth_tag):
    inner_prod = jnp.einsum(
        "gdi,gdj->gij", slot_real, slot_synth, preferred_element_type=jnp.float32
    )
    real_sq = jnp.sum(jnp.square(slot_real.astype(jnp.float32)), axis=1)
    synth_sq = jnp.sum(jnp.square(slot_synth.astype(jnp.float32)), axis=1)
    differ = (slot_real_tag[:, :, None] != slot_synth_tag[:, None, :]).astype(jnp.float32)
    return 0.5 * real_sq[:, :, None] + 0.5 * synth_sq[:, None, :] - inner_prod + PENALTY * differ


def lse_parts(scores, axis):
    highest = jnp.max(scores, axis=axis)
    mass_sum = jnp.sum(jnp.exp(scores - jnp.expand_dims(highest, axis)), axis=axis)
    return (highest, mass_sum)


def make_shards(n_blk, n_sub):
    def swap(value):
        return lax.ppermute(value, "sub", [(0, 1), (1, 0)])

    def partner(index, offset):
        if n_blk & (n_blk - 1) == 0:
            return index ^ offset
        return (index + offset) % n_blk

    def exchange(chunks, upward):
        moved = [chunks[0]]
        for offset in range(1, n_blk):
            if upward:
                perm = [(index, partner(index, offset)) for index in range(n_blk)]
            else:
                perm = [(partner(index, offset), index) for index in range(n_blk)]
            moved.append(lax.ppermute(chunks[offset], "blk", perm))
        return moved

    def send_up(chunks):
        return exchange(chunks, True)

    def send_down(chunks):
        return exchange(chunks, False)

    def shards(
        real_points,
        synth_points,
        real_cluster,
        synth_cluster,
        real_weight,
        synth_weight,
        pair_block,
        pair_row,
        pair_count,
    ):
        features, point_count = real_points.shape
        blocks = point_count // BLOCK
        marginals = real_weight.shape[0]
        half = marginals // n_sub
        peer_count, capacity = pair_block.shape
        wide = n_sub * capacity
        slot_count = peer_count * wide
        my_blk = lax.axis_index("blk")
        my_sub = lax.axis_index("sub")
        own_real = real_points.reshape(features, blocks, BLOCK)
        real_tags = real_cluster.reshape(1, blocks, BLOCK).astype(jnp.bfloat16)
        own_synth = jnp.concatenate(
            [synth_points, synth_cluster.astype(jnp.bfloat16)[None, :]], axis=0
        ).reshape(features + 1, blocks, BLOCK)
        log_real = jnp.log(
            lax.dynamic_slice_in_dim(real_weight, my_sub * half, half, 0).astype(jnp.float32) + 0.5
        ).reshape(half, blocks, BLOCK)
        log_synth = jnp.log(
            lax.dynamic_slice_in_dim(synth_weight, my_sub * half, half, 0).astype(jnp.float32) + 0.5
        ).reshape(half, blocks, BLOCK)

        offsets = jnp.arange(peer_count, dtype=jnp.int32)
        if peer_count & (peer_count - 1) == 0:
            peers = jnp.bitwise_xor(my_blk, offsets)
        else:
            peers = (my_blk + offsets) % peer_count
        half_points = point_count // n_sub
        own_half = lax.dynamic_slice_in_dim(
            own_synth.reshape(features + 1, point_count), my_sub * half_points, half_points, 1
        )
        arrived = send_down([own_half] * peer_count)[1:]
        other_half = swap(jnp.stack(arrived))
        everything = [own_synth]
        for index, mine in enumerate(arrived):
            low = jnp.where(my_sub == 0, mine, other_half[index])
            high = jnp.where(my_sub == 0, other_half[index], mine)
            everything.append(jnp.concatenate([low, high], axis=1).reshape(features + 1, blocks, BLOCK))
        lists = jnp.stack([pair_block, pair_row, jnp.broadcast_to(pair_count[:, None], pair_block.shape)])
        lists = jnp.stack([lists, swap(lists)], axis=1)
        listed = lax.broadcasted_iota(jnp.int32, lists.shape[1:], 2) < lists[2]
        wanted = pick_lead(jnp.transpose(jnp.where(listed, lists[0], 0), (1, 0, 2)), peers)
        rows_used = pick_lead(jnp.transpose(jnp.where(listed, lists[1], 0), (1, 0, 2)), peers)
        usable = pick_lead(jnp.transpose(listed.astype(jnp.int32), (1, 0, 2)), peers)
        wanted = wanted.reshape(peer_count, wide)
        rows_used = rows_used.reshape(slot_count)
        usable = usable.reshape(slot_count)[:, None, None] > 0
        far = jnp.concatenate(
            [pick_rows(everything[offset], wanted[offset], blocks) for offset in range(peer_count)], axis=0
        )
        far_y = far[:, :features]
        far_tags = far[:, features]
        slot_x = pick_rows(own_real, rows_used, blocks)
        slot_tags = pick_rows(real_tags, rows_used, blocks)[:, 0]
        cost_cols = slot_costs(slot_x, slot_tags, far_y, far_tags) / SMOOTH
        cost_rows = slot_costs(far_y, far_tags, slot_x, slot_tags) / SMOOTH

        synth_pot = jnp.zeros((half, blocks, BLOCK), jnp.float32)
        real_pot = jnp.zeros((half, blocks, BLOCK), jnp.float32)
        for sweep_index in range(ITERS):
            if sweep_index == 0:
                panel = jnp.zeros((slot_count, 1, BLOCK), jnp.float32)
            else:
                panel = jnp.concatenate(
                    send_down(
                        [
                            pick_rows(synth_pot, requested[offset * wide : (offset + 1) * wide], blocks)
                            for offset in range(peer_count)
                        ]
                    ),
                    axis=0,
                )
            highest, mass_sum = [], []
            for offset in range(peer_count):
                piece = slice(offset * wide, (offset + 1) * wide)
                scores = (panel[piece] / SMOOTH)[:, :, :, None] - cost_rows[piece, None]
                parts = lse_parts(scores, 2)
                highest.append(parts[0])
                mass_sum.append(parts[1])
            highest = jnp.concatenate(highest, axis=0)
            mass_sum = jnp.concatenate(mass_sum, axis=0)
            highest = jnp.where(usable, highest, SENTINEL)
            mass_sum = jnp.where(usable, mass_sum, 0.0)
            block_top, summed = fold_blocks(highest, mass_sum, rows_used, blocks)
            real_pot = finish(log_real, block_top, summed)

            own_rows = pick_rows(real_pot, rows_used, blocks)
            chunks = [None] * peer_count
            for offset in list(range(1, peer_count)) + [0]:
                piece = slice(offset * wide, (offset + 1) * wide)
                scores = (own_rows[piece] / SMOOTH)[:, :, :, None] - cost_cols[piece, None]
                highest, mass_sum = lse_parts(scores, 2)
                lse = jnp.where(usable[piece], highest + jnp.log(mass_sum), SENTINEL)
                if sweep_index == 0:
                    block_ids = jnp.broadcast_to(
                        wanted[offset].reshape(wide, 1, 1).astype(jnp.float32), (wide, 1, BLOCK)
                    )
                    lse = jnp.concatenate([lse, block_ids], axis=1)
                chunks[offset] = lse
            back = jnp.concatenate(send_up(chunks), axis=0)
            if sweep_index == 0:
                requested = back[:, half, 0].astype(jnp.int32)
                back = back[:, :half]
            block_top, summed = fold_lse(back, requested, blocks)
            synth_pot = finish(log_synth, block_top, summed)

        def both_halves(mine):
            other = swap(mine)
            first = jnp.where(my_sub == 0, mine, other)
            second = jnp.where(my_sub == 0, other, mine)
            return jnp.concatenate([first, second], axis=0).reshape(marginals, point_count)

        return (both_halves(real_pot), both_halves(synth_pot))

    return shards


def solution(mesh):
    placed = (
        P(None, ("slab", "blk")),
        P(None, ("slab", "blk")),
        P(("slab", "blk")),
        P(("slab", "blk")),
        P("bag", ("slab", "blk")),
        P("bag", ("slab", "blk")),
        P(("slab", "blk", "sub"), None),
        P(("slab", "blk", "sub"), None),
        P(("slab", "blk", "sub")),
    )
    return jax.shard_map(
        make_shards(mesh.shape["blk"], mesh.shape["sub"]),
        mesh=mesh,
        in_specs=placed,
        out_specs=(P("bag", ("slab", "blk")), P("bag", ("slab", "blk"))),
        check_vma=False,
    )
```

```python
import jax
import jax.numpy as jnp
from jax import lax
from jax.sharding import PartitionSpec as P

BLOCK = 128
ITERS = 2


SMOOTH = 0.1
PENALTY = 0.3
SENTINEL = -1e30


def join_parts(earlier, latter):
    larger = jnp.maximum(earlier[0], latter[0])
    return (
        larger,
        earlier[1] * jnp.exp(earlier[0] - larger) + latter[1] * jnp.exp(latter[0] - larger),
    )


def pick_rows(values, ids, blocks):
    hits = ids[:, None] == jnp.arange(blocks, dtype=jnp.int32)[None, :]
    chosen = jnp.where(hits[:, None, :, None], values[None], jnp.zeros((), values.dtype))
    return jnp.sum(chosen, axis=2, dtype=values.dtype)


def pick_lead(values, ids):
    hits = ids[:, None] == jnp.arange(values.shape[0], dtype=jnp.int32)[None, :]
    hits = hits.reshape(hits.shape + (1,) * (values.ndim - 1))
    return jnp.sum(jnp.where(hits, values[None], jnp.zeros((), values.dtype)), axis=1, dtype=values.dtype)


def fold_blocks(highest, mass_sum, owners, blocks):
    matches = owners[:, None] == jnp.arange(blocks, dtype=jnp.int32)[None, :]
    match_mask = matches[:, None, :, None]
    block_top = jnp.max(jnp.where(match_mask, highest[:, :, None, :], SENTINEL), axis=0)
    slot_top = pick_rows(block_top, owners, blocks)
    scaled = mass_sum * jnp.exp(highest - slot_top)
    summed = jnp.sum(jnp.where(match_mask, scaled[:, :, None, :], 0.0), axis=0)
    return (block_top, summed)


def fold_lse(lse, owners, blocks):
    matches = owners[:, None] == jnp.arange(blocks, dtype=jnp.int32)[None, :]
    match_mask = matches[:, None, :, None]
    block_top = jnp.max(jnp.where(match_mask, lse[:, :, None, :], SENTINEL), axis=0)
    slot_top = pick_rows(block_top, owners, blocks)
    scaled = jnp.where(lse > 0.5 * SENTINEL, jnp.exp(lse - slot_top), 0.0)
    summed = jnp.sum(jnp.where(match_mask, scaled[:, :, None, :], 0.0), axis=0)
    return (block_top, summed)


def finish(log_weight, block_top, summed):
    spread = jnp.where(summed > 0.5, block_top + jnp.log(jnp.maximum(summed, 0.5)), 0.0)
    return SMOOTH * log_weight - SMOOTH * spread


def slot_costs(slot_real, slot_real_tag, slot_synth, slot_synth_tag):
    inner_prod = jnp.einsum(
        "gdi,gdj->gij", slot_real, slot_synth, preferred_element_type=jnp.float32
    )
    real_sq = jnp.sum(jnp.square(slot_real.astype(jnp.float32)), axis=1)
    synth_sq = jnp.sum(jnp.square(slot_synth.astype(jnp.float32)), axis=1)
    differ = (slot_real_tag[:, :, None] != slot_synth_tag[:, None, :]).astype(jnp.float32)
    return 0.5 * real_sq[:, :, None] + 0.5 * synth_sq[:, None, :] - inner_prod + PENALTY * differ


def lse_parts(scores, axis):
    highest = jnp.max(scores, axis=axis)
    mass_sum = jnp.sum(jnp.exp(scores - jnp.expand_dims(highest, axis)), axis=axis)
    return (highest, mass_sum)


def make_shards(n_blk, n_sub):
    def swap(value):
        return lax.ppermute(value, "sub", [(0, 1), (1, 0)])

    def partner(index, offset):
        if n_blk & (n_blk - 1) == 0:
            return index ^ offset
        return (index + offset) % n_blk

    def exchange(chunks, upward):
        moved = [chunks[0]]
        for offset in range(1, n_blk):
            if upward:
                perm = [(index, partner(index, offset)) for index in range(n_blk)]
            else:
                perm = [(partner(index, offset), index) for index in range(n_blk)]
            moved.append(lax.ppermute(chunks[offset], "blk", perm))
        return moved

    def send_up(chunks):
        return exchange(chunks, True)

    def send_down(chunks):
        return exchange(chunks, False)

    def shards(
        real_points,
        synth_points,
        real_cluster,
        synth_cluster,
        real_weight,
        synth_weight,
        pair_block,
        pair_row,
        pair_count,
    ):
        features, point_count = real_points.shape
        blocks = point_count // BLOCK
        marginals = real_weight.shape[0]
        half = marginals // n_sub
        peer_count, capacity = pair_block.shape
        wide = n_sub * capacity
        slot_count = peer_count * wide
        my_blk = lax.axis_index("blk")
        my_sub = lax.axis_index("sub")
        own_real = real_points.reshape(features, blocks, BLOCK)
        real_tags = real_cluster.reshape(1, blocks, BLOCK).astype(jnp.bfloat16)
        own_synth = jnp.concatenate(
            [synth_points, synth_cluster.astype(jnp.bfloat16)[None, :]], axis=0
        ).reshape(features + 1, blocks, BLOCK)
        log_real = jnp.log(
            lax.dynamic_slice_in_dim(real_weight, my_sub * half, half, 0).astype(jnp.float32) + 0.5
        ).reshape(half, blocks, BLOCK)
        log_synth = jnp.log(
            lax.dynamic_slice_in_dim(synth_weight, my_sub * half, half, 0).astype(jnp.float32) + 0.5
        ).reshape(half, blocks, BLOCK)

        offsets = jnp.arange(peer_count, dtype=jnp.int32)
        if peer_count & (peer_count - 1) == 0:
            peers = jnp.bitwise_xor(my_blk, offsets)
        else:
            peers = (my_blk + offsets) % peer_count
        everything = send_down([own_synth] * peer_count)
        lists = jnp.stack([pair_block, pair_row, jnp.broadcast_to(pair_count[:, None], pair_block.shape)])
        lists = jnp.stack([lists, swap(lists)], axis=1)
        listed = lax.broadcasted_iota(jnp.int32, lists.shape[1:], 2) < lists[2]
        wanted = pick_lead(jnp.transpose(jnp.where(listed, lists[0], 0), (1, 0, 2)), peers)
        rows_used = pick_lead(jnp.transpose(jnp.where(listed, lists[1], 0), (1, 0, 2)), peers)
        usable = pick_lead(jnp.transpose(listed.astype(jnp.int32), (1, 0, 2)), peers)
        wanted = wanted.reshape(peer_count, wide)
        rows_used = rows_used.reshape(slot_count)
        usable = usable.reshape(slot_count)[:, None, None] > 0
        far = jnp.concatenate(
            [pick_rows(everything[offset], wanted[offset], blocks) for offset in range(peer_count)], axis=0
        )
        far_y = far[:, :features]
        far_tags = far[:, features]
        slot_x = pick_rows(own_real, rows_used, blocks)
        slot_tags = pick_rows(real_tags, rows_used, blocks)[:, 0]
        cost_cols = slot_costs(slot_x, slot_tags, far_y, far_tags) / SMOOTH
        cost_rows = slot_costs(far_y, far_tags, slot_x, slot_tags) / SMOOTH

        synth_pot = jnp.zeros((half, blocks, BLOCK), jnp.float32)
        real_pot = jnp.zeros((half, blocks, BLOCK), jnp.float32)
        for sweep_index in range(ITERS):
            if sweep_index == 0:
                panels = [jnp.zeros((wide, 1, BLOCK), jnp.float32)] * peer_count
            else:
                arrived = send_down([synth_pot] * peer_count)
                panels = [pick_rows(arrived[offset], wanted[offset], blocks) for offset in range(peer_count)]
            highest, mass_sum = [], []
            for offset in range(peer_count):
                piece = slice(offset * wide, (offset + 1) * wide)
                scores = (panels[offset] / SMOOTH)[:, :, :, None] - cost_rows[piece, None]
                parts = lse_parts(scores, 2)
                highest.append(parts[0])
                mass_sum.append(parts[1])
            highest = jnp.concatenate(highest, axis=0)
            mass_sum = jnp.concatenate(mass_sum, axis=0)
            highest = jnp.where(usable, highest, SENTINEL)
            mass_sum = jnp.where(usable, mass_sum, 0.0)
            block_top, summed = fold_blocks(highest, mass_sum, rows_used, blocks)
            real_pot = finish(log_real, block_top, summed)

            own_rows = pick_rows(real_pot, rows_used, blocks)
            chunks = [None] * peer_count
            for offset in list(range(1, peer_count)) + [0]:
                piece = slice(offset * wide, (offset + 1) * wide)
                scores = (own_rows[piece] / SMOOTH)[:, :, :, None] - cost_cols[piece, None]
                highest, mass_sum = lse_parts(scores, 2)
                lse = jnp.where(usable[piece], highest + jnp.log(mass_sum), SENTINEL)
                if sweep_index == 0:
                    block_ids = jnp.broadcast_to(
                        wanted[offset].reshape(wide, 1, 1).astype(jnp.float32), (wide, 1, BLOCK)
                    )
                    lse = jnp.concatenate([lse, block_ids], axis=1)
                chunks[offset] = lse
            back = jnp.concatenate(send_up(chunks), axis=0)
            if sweep_index == 0:
                requested = back[:, half, 0].astype(jnp.int32)
                back = back[:, :half]
            block_top, summed = fold_lse(back, requested, blocks)
            synth_pot = finish(log_synth, block_top, summed)

        def both_halves(mine):
            other = swap(mine)
            first = jnp.where(my_sub == 0, mine, other)
            second = jnp.where(my_sub == 0, other, mine)
            return jnp.concatenate([first, second], axis=0).reshape(marginals, point_count)

        return (both_halves(real_pot), both_halves(synth_pot))

    return shards


def solution(mesh):
    placed = (
        P(None, ("slab", "blk")),
        P(None, ("slab", "blk")),
        P(("slab", "blk")),
        P(("slab", "blk")),
        P("bag", ("slab", "blk")),
        P("bag", ("slab", "blk")),
        P(("slab", "blk", "sub"), None),
        P(("slab", "blk", "sub"), None),
        P(("slab", "blk", "sub")),
    )
    return jax.shard_map(
        make_shards(mesh.shape["blk"], mesh.shape["sub"]),
        mesh=mesh,
        in_specs=placed,
        out_specs=(P("bag", ("slab", "blk")), P("bag", ("slab", "blk"))),
        check_vma=False,
    )
```

```python
import jax
import jax.numpy as jnp
from jax import lax
from jax.sharding import PartitionSpec as P

BLOCK = 128
ITERS = 2


SMOOTH = 0.1
PENALTY = 0.3
SENTINEL = -1e30


def join_parts(earlier, latter):
    larger = jnp.maximum(earlier[0], latter[0])
    return (
        larger,
        earlier[1] * jnp.exp(earlier[0] - larger) + latter[1] * jnp.exp(latter[0] - larger),
    )


def pick_rows(values, ids, blocks):
    hits = ids[:, None] == jnp.arange(blocks, dtype=jnp.int32)[None, :]
    chosen = jnp.where(hits[:, None, :, None], values[None], jnp.zeros((), values.dtype))
    return jnp.sum(chosen, axis=2, dtype=values.dtype)


def pick_lead(values, ids):
    hits = ids[:, None] == jnp.arange(values.shape[0], dtype=jnp.int32)[None, :]
    hits = hits.reshape(hits.shape + (1,) * (values.ndim - 1))
    return jnp.sum(jnp.where(hits, values[None], jnp.zeros((), values.dtype)), axis=1, dtype=values.dtype)


def fold_blocks(highest, mass_sum, owners, blocks):
    matches = owners[:, None] == jnp.arange(blocks, dtype=jnp.int32)[None, :]
    match_mask = matches[:, None, :, None]
    block_top = jnp.max(jnp.where(match_mask, highest[:, :, None, :], SENTINEL), axis=0)
    slot_top = pick_rows(block_top, owners, blocks)
    scaled = mass_sum * jnp.exp(highest - slot_top)
    summed = jnp.sum(jnp.where(match_mask, scaled[:, :, None, :], 0.0), axis=0)
    return (block_top, summed)


def fold_lse(lse, owners, blocks):
    matches = owners[:, None] == jnp.arange(blocks, dtype=jnp.int32)[None, :]
    match_mask = matches[:, None, :, None]
    block_top = jnp.max(jnp.where(match_mask, lse[:, :, None, :], SENTINEL), axis=0)
    slot_top = pick_rows(block_top, owners, blocks)
    scaled = jnp.where(lse > 0.5 * SENTINEL, jnp.exp(lse - slot_top), 0.0)
    summed = jnp.sum(jnp.where(match_mask, scaled[:, :, None, :], 0.0), axis=0)
    return (block_top, summed)


def finish(log_weight, block_top, summed):
    spread = jnp.where(summed > 0.5, block_top + jnp.log(jnp.maximum(summed, 0.5)), 0.0)
    return SMOOTH * log_weight - SMOOTH * spread


def slot_costs(slot_real, slot_real_tag, slot_synth, slot_synth_tag):
    inner_prod = jnp.einsum(
        "gdi,gdj->gij", slot_real, slot_synth, preferred_element_type=jnp.float32
    )
    real_sq = jnp.sum(jnp.square(slot_real.astype(jnp.float32)), axis=1)
    synth_sq = jnp.sum(jnp.square(slot_synth.astype(jnp.float32)), axis=1)
    differ = (slot_real_tag[:, :, None] != slot_synth_tag[:, None, :]).astype(jnp.float32)
    return 0.5 * real_sq[:, :, None] + 0.5 * synth_sq[:, None, :] - inner_prod + PENALTY * differ


def lse_parts(scores, axis):
    highest = jnp.max(scores, axis=axis)
    mass_sum = jnp.sum(jnp.exp(scores - jnp.expand_dims(highest, axis)), axis=axis)
    return (highest, mass_sum)


def make_shards(n_blk, n_sub):
    def swap(value):
        return lax.ppermute(value, "sub", [(0, 1), (1, 0)])

    def partner(index, offset):
        if n_blk & (n_blk - 1) == 0:
            return index ^ offset
        return (index + offset) % n_blk

    def exchange(chunks, upward):
        moved = [chunks[0]]
        for offset in range(1, n_blk):
            if upward:
                perm = [(index, partner(index, offset)) for index in range(n_blk)]
            else:
                perm = [(partner(index, offset), index) for index in range(n_blk)]
            moved.append(lax.ppermute(chunks[offset], "blk", perm))
        return moved

    def send_up(chunks):
        return exchange(chunks, True)

    def send_down(chunks):
        return exchange(chunks, False)

    def shards(
        real_points,
        synth_points,
        real_cluster,
        synth_cluster,
        real_weight,
        synth_weight,
        pair_block,
        pair_row,
        pair_count,
    ):
        features, point_count = real_points.shape
        blocks = point_count // BLOCK
        marginals = real_weight.shape[0]
        half = marginals // n_sub
        peer_count, capacity = pair_block.shape
        wide = n_sub * capacity
        slot_count = peer_count * wide
        my_blk = lax.axis_index("blk")
        my_sub = lax.axis_index("sub")
        own_real = real_points.reshape(features, blocks, BLOCK)
        real_tags = real_cluster.reshape(1, blocks, BLOCK).astype(jnp.bfloat16)
        own_synth = jnp.concatenate(
            [synth_points, synth_cluster.astype(jnp.bfloat16)[None, :]], axis=0
        ).reshape(features + 1, blocks, BLOCK)
        log_real = jnp.log(
            lax.dynamic_slice_in_dim(real_weight, my_sub * half, half, 0).astype(jnp.float32) + 0.5
        ).reshape(half, blocks, BLOCK)
        log_synth = jnp.log(
            lax.dynamic_slice_in_dim(synth_weight, my_sub * half, half, 0).astype(jnp.float32) + 0.5
        ).reshape(half, blocks, BLOCK)

        offsets = jnp.arange(peer_count, dtype=jnp.int32)
        if peer_count & (peer_count - 1) == 0:
            peers = jnp.bitwise_xor(my_blk, offsets)
        else:
            peers = (my_blk + offsets) % peer_count
        everything = send_down([own_synth] * peer_count)
        lists = jnp.stack([pair_block, pair_row, jnp.broadcast_to(pair_count[:, None], pair_block.shape)])
        lists = jnp.stack([lists, swap(lists)], axis=1)
        listed = lax.broadcasted_iota(jnp.int32, lists.shape[1:], 2) < lists[2]
        wanted = pick_lead(jnp.transpose(jnp.where(listed, lists[0], 0), (1, 0, 2)), peers)
        rows_used = pick_lead(jnp.transpose(jnp.where(listed, lists[1], 0), (1, 0, 2)), peers)
        usable = pick_lead(jnp.transpose(listed.astype(jnp.int32), (1, 0, 2)), peers)
        wanted = wanted.reshape(peer_count, wide)
        rows_used = rows_used.reshape(slot_count)
        usable = usable.reshape(slot_count)[:, None, None] > 0
        far = jnp.concatenate(
            [pick_rows(everything[offset], wanted[offset], blocks) for offset in range(peer_count)], axis=0
        )
        far_y = far[:, :features]
        far_tags = far[:, features]
        slot_x = pick_rows(own_real, rows_used, blocks)
        slot_tags = pick_rows(real_tags, rows_used, blocks)[:, 0]
        cost_cols = slot_costs(slot_x, slot_tags, far_y, far_tags) / SMOOTH
        cost_rows = slot_costs(far_y, far_tags, slot_x, slot_tags) / SMOOTH

        synth_pot = jnp.zeros((half, blocks, BLOCK), jnp.float32)
        real_pot = jnp.zeros((half, blocks, BLOCK), jnp.float32)
        for sweep_index in range(ITERS):
            if sweep_index == 0:
                panel = jnp.zeros((slot_count, 1, BLOCK), jnp.float32)
            else:
                panel = jnp.concatenate(
                    send_down(
                        [
                            pick_rows(synth_pot, requested[offset * wide : (offset + 1) * wide], blocks)
                            for offset in range(peer_count)
                        ]
                    ),
                    axis=0,
                )
            if sweep_index == 0:
                highest, mass_sum = lse_parts(0.0 - cost_cols[:, None], 3)
            else:
                highest, mass_sum = [], []
                for offset in range(peer_count):
                    piece = slice(offset * wide, (offset + 1) * wide)
                    scores = (panel[piece] / SMOOTH)[:, :, :, None] - cost_rows[piece, None]
                    parts = lse_parts(scores, 2)
                    highest.append(parts[0])
                    mass_sum.append(parts[1])
                highest = jnp.concatenate(highest, axis=0)
                mass_sum = jnp.concatenate(mass_sum, axis=0)
            highest = jnp.where(usable, highest, SENTINEL)
            mass_sum = jnp.where(usable, mass_sum, 0.0)
            block_top, summed = fold_blocks(highest, mass_sum, rows_used, blocks)
            real_pot = finish(log_real, block_top, summed)

            own_rows = pick_rows(real_pot, rows_used, blocks)
            chunks = [None] * peer_count
            for offset in list(range(1, peer_count)) + [0]:
                piece = slice(offset * wide, (offset + 1) * wide)
                scores = (own_rows[piece] / SMOOTH)[:, :, :, None] - cost_cols[piece, None]
                highest, mass_sum = lse_parts(scores, 2)
                lse = jnp.where(usable[piece], highest + jnp.log(mass_sum), SENTINEL)
                if sweep_index == 0:
                    block_ids = jnp.broadcast_to(
                        wanted[offset].reshape(wide, 1, 1).astype(jnp.float32), (wide, 1, BLOCK)
                    )
                    lse = jnp.concatenate([lse, block_ids], axis=1)
                chunks[offset] = lse
            back = jnp.concatenate(send_up(chunks), axis=0)
            if sweep_index == 0:
                requested = back[:, half, 0].astype(jnp.int32)
                back = back[:, :half]
            block_top, summed = fold_lse(back, requested, blocks)
            synth_pot = finish(log_synth, block_top, summed)

        def both_halves(mine):
            other = swap(mine)
            first = jnp.where(my_sub == 0, mine, other)
            second = jnp.where(my_sub == 0, other, mine)
            return jnp.concatenate([first, second], axis=0).reshape(marginals, point_count)

        return (both_halves(real_pot), both_halves(synth_pot))

    return shards


def solution(mesh):
    placed = (
        P(None, ("slab", "blk")),
        P(None, ("slab", "blk")),
        P(("slab", "blk")),
        P(("slab", "blk")),
        P("bag", ("slab", "blk")),
        P("bag", ("slab", "blk")),
        P(("slab", "blk", "sub"), None),
        P(("slab", "blk", "sub"), None),
        P(("slab", "blk", "sub")),
    )
    return jax.shard_map(
        make_shards(mesh.shape["blk"], mesh.shape["sub"]),
        mesh=mesh,
        in_specs=placed,
        out_specs=(P("bag", ("slab", "blk")), P("bag", ("slab", "blk"))),
        check_vma=False,
    )
```

```python
import jax
import jax.numpy as jnp
from jax import lax
from jax.sharding import PartitionSpec as P

BLOCK = 128
ITERS = 2


SMOOTH = 0.1
PENALTY = 0.3
SENTINEL = -1e30


def join_parts(earlier, latter):
    larger = jnp.maximum(earlier[0], latter[0])
    return (
        larger,
        earlier[1] * jnp.exp(earlier[0] - larger) + latter[1] * jnp.exp(latter[0] - larger),
    )


def pick_rows(values, ids, blocks):
    hits = ids[:, None] == jnp.arange(blocks, dtype=jnp.int32)[None, :]
    chosen = jnp.where(hits[:, None, :, None], values[None], jnp.zeros((), values.dtype))
    return jnp.sum(chosen, axis=2, dtype=values.dtype)


def pick_lead(values, ids):
    hits = ids[:, None] == jnp.arange(values.shape[0], dtype=jnp.int32)[None, :]
    hits = hits.reshape(hits.shape + (1,) * (values.ndim - 1))
    return jnp.sum(jnp.where(hits, values[None], jnp.zeros((), values.dtype)), axis=1, dtype=values.dtype)


def fold_blocks(highest, mass_sum, owners, blocks):
    matches = owners[:, None] == jnp.arange(blocks, dtype=jnp.int32)[None, :]
    match_mask = matches[:, None, :, None]
    block_top = jnp.max(jnp.where(match_mask, highest[:, :, None, :], SENTINEL), axis=0)
    slot_top = pick_rows(block_top, owners, blocks)
    scaled = mass_sum * jnp.exp(highest - slot_top)
    summed = jnp.sum(jnp.where(match_mask, scaled[:, :, None, :], 0.0), axis=0)
    return (block_top, summed)


def fold_lse(lse, owners, blocks):
    matches = owners[:, None] == jnp.arange(blocks, dtype=jnp.int32)[None, :]
    match_mask = matches[:, None, :, None]
    block_top = jnp.max(jnp.where(match_mask, lse[:, :, None, :], SENTINEL), axis=0)
    slot_top = pick_rows(block_top, owners, blocks)
    scaled = jnp.where(lse > 0.5 * SENTINEL, jnp.exp(lse - slot_top), 0.0)
    summed = jnp.sum(jnp.where(match_mask, scaled[:, :, None, :], 0.0), axis=0)
    return (block_top, summed)


def finish(log_weight, block_top, summed):
    spread = jnp.where(summed > 0.5, block_top + jnp.log(jnp.maximum(summed, 0.5)), 0.0)
    return SMOOTH * log_weight - SMOOTH * spread


def slot_costs(slot_real, slot_real_tag, slot_synth, slot_synth_tag):
    inner_prod = jnp.einsum(
        "gdi,gdj->gij", slot_real, slot_synth, preferred_element_type=jnp.float32
    )
    real_sq = jnp.sum(jnp.square(slot_real.astype(jnp.float32)), axis=1)
    synth_sq = jnp.sum(jnp.square(slot_synth.astype(jnp.float32)), axis=1)
    differ = (slot_real_tag[:, :, None] != slot_synth_tag[:, None, :]).astype(jnp.float32)
    return 0.5 * real_sq[:, :, None] + 0.5 * synth_sq[:, None, :] - inner_prod + PENALTY * differ


def lse_parts(scores, axis):
    highest = jnp.max(scores, axis=axis)
    mass_sum = jnp.sum(jnp.exp(scores - jnp.expand_dims(highest, axis)), axis=axis)
    return (highest, mass_sum)


def make_shards(n_blk, n_sub):
    def swap(value):
        return lax.ppermute(value, "sub", [(0, 1), (1, 0)])

    def partner(index, offset):
        if n_blk & (n_blk - 1) == 0:
            return index ^ offset
        return (index + offset) % n_blk

    def exchange(chunks, upward):
        moved = [chunks[0]]
        for offset in range(1, n_blk):
            if upward:
                perm = [(index, partner(index, offset)) for index in range(n_blk)]
            else:
                perm = [(partner(index, offset), index) for index in range(n_blk)]
            moved.append(lax.ppermute(chunks[offset], "blk", perm))
        return moved

    def send_up(chunks):
        return exchange(chunks, True)

    def send_down(chunks):
        return exchange(chunks, False)

    def shards(
        real_points,
        synth_points,
        real_cluster,
        synth_cluster,
        real_weight,
        synth_weight,
        pair_block,
        pair_row,
        pair_count,
    ):
        features, point_count = real_points.shape
        blocks = point_count // BLOCK
        marginals = real_weight.shape[0]
        half = marginals // n_sub
        peer_count, capacity = pair_block.shape
        wide = n_sub * capacity
        slot_count = peer_count * wide
        my_blk = lax.axis_index("blk")
        my_sub = lax.axis_index("sub")
        own_real = real_points.reshape(features, blocks, BLOCK)
        real_tags = real_cluster.reshape(1, blocks, BLOCK).astype(jnp.bfloat16)
        own_synth = jnp.concatenate(
            [synth_points, synth_cluster.astype(jnp.bfloat16)[None, :]], axis=0
        ).reshape(features + 1, blocks, BLOCK)
        log_real = jnp.log(
            lax.dynamic_slice_in_dim(real_weight, my_sub * half, half, 0).astype(jnp.float32) + 0.5
        ).reshape(half, blocks, BLOCK)
        log_synth = jnp.log(
            lax.dynamic_slice_in_dim(synth_weight, my_sub * half, half, 0).astype(jnp.float32) + 0.5
        ).reshape(half, blocks, BLOCK)

        offsets = jnp.arange(peer_count, dtype=jnp.int32)
        if peer_count & (peer_count - 1) == 0:
            peers = jnp.bitwise_xor(my_blk, offsets)
        else:
            peers = (my_blk + offsets) % peer_count
        everything = send_down([own_synth] * peer_count)
        lists = jnp.stack([pair_block, pair_row, jnp.broadcast_to(pair_count[:, None], pair_block.shape)])
        lists = jnp.stack([lists, swap(lists)], axis=1)
        listed = lax.broadcasted_iota(jnp.int32, lists.shape[1:], 2) < lists[2]
        wanted = pick_lead(jnp.transpose(jnp.where(listed, lists[0], 0), (1, 0, 2)), peers)
        rows_used = pick_lead(jnp.transpose(jnp.where(listed, lists[1], 0), (1, 0, 2)), peers)
        usable = pick_lead(jnp.transpose(listed.astype(jnp.int32), (1, 0, 2)), peers)
        wanted = wanted.reshape(peer_count, wide)
        rows_used = rows_used.reshape(slot_count)
        usable = usable.reshape(slot_count)[:, None, None] > 0
        far = jnp.concatenate(
            [pick_rows(everything[offset], wanted[offset], blocks) for offset in range(peer_count)], axis=0
        )
        far_y = far[:, :features]
        far_tags = far[:, features]
        slot_x = pick_rows(own_real, rows_used, blocks)
        slot_tags = pick_rows(real_tags, rows_used, blocks)[:, 0]
        cost_cols = slot_costs(slot_x, slot_tags, far_y, far_tags) / SMOOTH
        cost_rows = slot_costs(far_y, far_tags, slot_x, slot_tags) / SMOOTH

        synth_pot = jnp.zeros((half, blocks, BLOCK), jnp.float32)
        real_pot = jnp.zeros((half, blocks, BLOCK), jnp.float32)
        for sweep_index in range(ITERS):
            if sweep_index == 0:
                panel = jnp.zeros((slot_count, 1, BLOCK), jnp.float32)
            else:
                panel = jnp.concatenate(
                    send_down(
                        [
                            pick_rows(synth_pot, requested[offset * wide : (offset + 1) * wide], blocks)
                            for offset in range(peer_count)
                        ]
                    ),
                    axis=0,
                )
            highest, mass_sum = [], []
            for offset in range(peer_count):
                piece = slice(offset * wide, (offset + 1) * wide)
                scores = (panel[piece] / SMOOTH)[:, :, :, None] - cost_rows[piece, None]
                parts = lse_parts(scores, 2)
                highest.append(parts[0])
                mass_sum.append(parts[1])
            highest = jnp.concatenate(highest, axis=0)
            mass_sum = jnp.concatenate(mass_sum, axis=0)
            highest = jnp.where(usable, highest, SENTINEL)
            mass_sum = jnp.where(usable, mass_sum, 0.0)
            block_top, summed = fold_blocks(highest, mass_sum, rows_used, blocks)
            real_pot = finish(log_real, block_top, summed)

            own_rows = pick_rows(real_pot, rows_used, blocks)
            chunks = [None] * peer_count
            for offset in list(range(1, peer_count)) + [0]:
                piece = slice(offset * wide, (offset + 1) * wide)
                scores = (own_rows[piece] / SMOOTH)[:, :, :, None] - cost_cols[piece, None]
                highest, mass_sum = lse_parts(scores, 2)
                lse = jnp.where(usable[piece], highest + jnp.log(mass_sum), SENTINEL)
                if sweep_index == 0:
                    block_ids = jnp.concatenate(
                        [wanted[offset].astype(jnp.float32)[None, :], jnp.zeros((1, BLOCK - wide), jnp.float32)],
                        axis=1,
                    )
                    lse = jnp.concatenate([lse.reshape(wide * half, BLOCK), block_ids], axis=0)
                chunks[offset] = lse
            moved = send_up(chunks)
            if sweep_index == 0:
                requested = jnp.concatenate(
                    [chunk[wide * half, :wide].astype(jnp.int32) for chunk in moved], axis=0
                )
                moved = [chunk[: wide * half].reshape(wide, half, BLOCK) for chunk in moved]
            back = jnp.concatenate(moved, axis=0)
            block_top, summed = fold_lse(back, requested, blocks)
            synth_pot = finish(log_synth, block_top, summed)

        def both_halves(mine):
            other = swap(mine)
            first = jnp.where(my_sub == 0, mine, other)
            second = jnp.where(my_sub == 0, other, mine)
            return jnp.concatenate([first, second], axis=0).reshape(marginals, point_count)

        return (both_halves(real_pot), both_halves(synth_pot))

    return shards


def solution(mesh):
    placed = (
        P(None, ("slab", "blk")),
        P(None, ("slab", "blk")),
        P(("slab", "blk")),
        P(("slab", "blk")),
        P("bag", ("slab", "blk")),
        P("bag", ("slab", "blk")),
        P(("slab", "blk", "sub"), None),
        P(("slab", "blk", "sub"), None),
        P(("slab", "blk", "sub")),
    )
    return jax.shard_map(
        make_shards(mesh.shape["blk"], mesh.shape["sub"]),
        mesh=mesh,
        in_specs=placed,
        out_specs=(P("bag", ("slab", "blk")), P("bag", ("slab", "blk"))),
        check_vma=False,
    )
```

```python
import jax
import jax.numpy as jnp
from jax import lax
from jax.sharding import PartitionSpec as P

BLOCK = 128
ITERS = 2


SMOOTH = 0.1
PENALTY = 0.3
SENTINEL = -1e30


def join_parts(earlier, latter):
    larger = jnp.maximum(earlier[0], latter[0])
    return (
        larger,
        earlier[1] * jnp.exp(earlier[0] - larger) + latter[1] * jnp.exp(latter[0] - larger),
    )


def pick_rows(values, ids, blocks):
    hits = ids[:, None] == jnp.arange(blocks, dtype=jnp.int32)[None, :]
    chosen = jnp.where(hits[:, None, :, None], values[None], jnp.zeros((), values.dtype))
    return jnp.sum(chosen, axis=2, dtype=values.dtype)


def pick_lead(values, ids):
    hits = ids[:, None] == jnp.arange(values.shape[0], dtype=jnp.int32)[None, :]
    hits = hits.reshape(hits.shape + (1,) * (values.ndim - 1))
    return jnp.sum(jnp.where(hits, values[None], jnp.zeros((), values.dtype)), axis=1, dtype=values.dtype)


def fold_blocks(highest, mass_sum, owners, blocks):
    matches = owners[:, None] == jnp.arange(blocks, dtype=jnp.int32)[None, :]
    match_mask = matches[:, None, :, None]
    block_top = jnp.max(jnp.where(match_mask, highest[:, :, None, :], SENTINEL), axis=0)
    slot_top = pick_rows(block_top, owners, blocks)
    scaled = mass_sum * jnp.exp(highest - slot_top)
    summed = jnp.sum(jnp.where(match_mask, scaled[:, :, None, :], 0.0), axis=0)
    return (block_top, summed)


def fold_lse(lse, owners, blocks):
    matches = owners[:, None] == jnp.arange(blocks, dtype=jnp.int32)[None, :]
    match_mask = matches[:, None, :, None]
    block_top = jnp.max(jnp.where(match_mask, lse[:, :, None, :], SENTINEL), axis=0)
    slot_top = pick_rows(block_top, owners, blocks)
    scaled = jnp.where(lse > 0.5 * SENTINEL, jnp.exp(lse - slot_top), 0.0)
    summed = jnp.sum(jnp.where(match_mask, scaled[:, :, None, :], 0.0), axis=0)
    return (block_top, summed)


def finish(log_weight, block_top, summed):
    spread = jnp.where(summed > 0.5, block_top + jnp.log(jnp.maximum(summed, 0.5)), 0.0)
    return SMOOTH * log_weight - SMOOTH * spread


def slot_costs(slot_real, slot_real_tag, slot_synth, slot_synth_tag):
    inner_prod = jnp.einsum(
        "gdi,gdj->gij", slot_real, slot_synth, preferred_element_type=jnp.float32
    )
    real_sq = jnp.sum(jnp.square(slot_real.astype(jnp.float32)), axis=1)
    synth_sq = jnp.sum(jnp.square(slot_synth.astype(jnp.float32)), axis=1)
    differ = (slot_real_tag[:, :, None] != slot_synth_tag[:, None, :]).astype(jnp.float32)
    return 0.5 * real_sq[:, :, None] + 0.5 * synth_sq[:, None, :] - inner_prod + PENALTY * differ


def lse_parts(scores, axis):
    highest = jnp.max(scores, axis=axis)
    mass_sum = jnp.sum(jnp.exp(scores - jnp.expand_dims(highest, axis)), axis=axis)
    return (highest, mass_sum)


def make_shards(n_blk, n_sub):
    def swap(value):
        return lax.ppermute(value, "sub", [(0, 1), (1, 0)])

    def partner(index, offset):
        if n_blk & (n_blk - 1) == 0:
            return index ^ offset
        return (index + offset) % n_blk

    def exchange(chunks, upward):
        moved = [chunks[0]]
        for offset in range(1, n_blk):
            if upward:
                perm = [(index, partner(index, offset)) for index in range(n_blk)]
            else:
                perm = [(partner(index, offset), index) for index in range(n_blk)]
            moved.append(lax.ppermute(chunks[offset], "blk", perm))
        return moved

    def send_up(chunks):
        return exchange(chunks, True)

    def send_down(chunks):
        return exchange(chunks, False)

    def shards(
        real_points,
        synth_points,
        real_cluster,
        synth_cluster,
        real_weight,
        synth_weight,
        pair_block,
        pair_row,
        pair_count,
    ):
        features, point_count = real_points.shape
        blocks = point_count // BLOCK
        marginals = real_weight.shape[0]
        half = marginals // n_sub
        peer_count, capacity = pair_block.shape
        wide = n_sub * capacity
        slot_count = peer_count * wide
        my_blk = lax.axis_index("blk")
        my_sub = lax.axis_index("sub")
        own_real = real_points.reshape(features, blocks, BLOCK)
        real_tags = real_cluster.reshape(1, blocks, BLOCK).astype(jnp.bfloat16)
        own_synth = jnp.concatenate([synth_points, synth_cluster.astype(jnp.bfloat16)[None, :]], axis=0)
        log_real = jnp.log(
            lax.dynamic_slice_in_dim(real_weight, my_sub * half, half, 0).astype(jnp.float32) + 0.5
        ).reshape(half, blocks, BLOCK)
        log_synth = jnp.log(
            lax.dynamic_slice_in_dim(synth_weight, my_sub * half, half, 0).astype(jnp.float32) + 0.5
        ).reshape(half, blocks, BLOCK)

        offsets = jnp.arange(peer_count, dtype=jnp.int32)
        if peer_count & (peer_count - 1) == 0:
            peers = jnp.bitwise_xor(my_blk, offsets)
        else:
            peers = (my_blk + offsets) % peer_count
        everything = send_down([own_synth] * peer_count)
        lists = jnp.stack([pair_block, pair_row, jnp.broadcast_to(pair_count[:, None], pair_block.shape)])
        lists = jnp.stack([lists, swap(lists)], axis=1)
        listed = lax.broadcasted_iota(jnp.int32, lists.shape[1:], 2) < lists[2]
        wanted = pick_lead(jnp.transpose(jnp.where(listed, lists[0], 0), (1, 0, 2)), peers)
        rows_used = pick_lead(jnp.transpose(jnp.where(listed, lists[1], 0), (1, 0, 2)), peers)
        usable = pick_lead(jnp.transpose(listed.astype(jnp.int32), (1, 0, 2)), peers)
        wanted = wanted.reshape(peer_count, wide)
        rows_used = rows_used.reshape(slot_count)
        usable = usable.reshape(slot_count)[:, None, None] > 0
        far = jnp.concatenate(
            [
                pick_rows(everything[offset].reshape(features + 1, blocks, BLOCK), wanted[offset], blocks)
                for offset in range(peer_count)
            ],
            axis=0,
        )
        far_y = far[:, :features]
        far_tags = far[:, features]
        slot_x = pick_rows(own_real, rows_used, blocks)
        slot_tags = pick_rows(real_tags, rows_used, blocks)[:, 0]
        cost_cols = slot_costs(slot_x, slot_tags, far_y, far_tags) / SMOOTH
        cost_rows = slot_costs(far_y, far_tags, slot_x, slot_tags) / SMOOTH

        synth_pot = jnp.zeros((half, blocks, BLOCK), jnp.float32)
        real_pot = jnp.zeros((half, blocks, BLOCK), jnp.float32)
        for sweep_index in range(ITERS):
            if sweep_index == 0:
                panel = jnp.zeros((slot_count, 1, BLOCK), jnp.float32)
            else:
                panel = jnp.concatenate(
                    send_down(
                        [
                            pick_rows(synth_pot, requested[offset * wide : (offset + 1) * wide], blocks)
                            for offset in range(peer_count)
                        ]
                    ),
                    axis=0,
                )
            highest, mass_sum = [], []
            for offset in range(peer_count):
                piece = slice(offset * wide, (offset + 1) * wide)
                scores = (panel[piece] / SMOOTH)[:, :, :, None] - cost_rows[piece, None]
                parts = lse_parts(scores, 2)
                highest.append(parts[0])
                mass_sum.append(parts[1])
            highest = jnp.concatenate(highest, axis=0)
            mass_sum = jnp.concatenate(mass_sum, axis=0)
            highest = jnp.where(usable, highest, SENTINEL)
            mass_sum = jnp.where(usable, mass_sum, 0.0)
            block_top, summed = fold_blocks(highest, mass_sum, rows_used, blocks)
            real_pot = finish(log_real, block_top, summed)

            own_rows = pick_rows(real_pot, rows_used, blocks)
            chunks = [None] * peer_count
            for offset in list(range(1, peer_count)) + [0]:
                piece = slice(offset * wide, (offset + 1) * wide)
                scores = (own_rows[piece] / SMOOTH)[:, :, :, None] - cost_cols[piece, None]
                highest, mass_sum = lse_parts(scores, 2)
                lse = jnp.where(usable[piece], highest + jnp.log(mass_sum), SENTINEL)
                if sweep_index == 0:
                    block_ids = jnp.concatenate(
                        [wanted[offset].astype(jnp.float32)[None, :], jnp.zeros((1, BLOCK - wide), jnp.float32)],
                        axis=1,
                    )
                    lse = jnp.concatenate([lse.reshape(wide * half, BLOCK), block_ids], axis=0)
                chunks[offset] = lse
            moved = send_up(chunks)
            if sweep_index == 0:
                requested = jnp.concatenate(
                    [chunk[wide * half, :wide].astype(jnp.int32) for chunk in moved], axis=0
                )
                moved = [chunk[: wide * half].reshape(wide, half, BLOCK) for chunk in moved]
            back = jnp.concatenate(moved, axis=0)
            block_top, summed = fold_lse(back, requested, blocks)
            synth_pot = finish(log_synth, block_top, summed)

        def both_halves(mine):
            other = swap(mine)
            first = jnp.where(my_sub == 0, mine, other)
            second = jnp.where(my_sub == 0, other, mine)
            return jnp.concatenate([first, second], axis=0).reshape(marginals, point_count)

        return (both_halves(real_pot), both_halves(synth_pot))

    return shards


def solution(mesh):
    placed = (
        P(None, ("slab", "blk")),
        P(None, ("slab", "blk")),
        P(("slab", "blk")),
        P(("slab", "blk")),
        P("bag", ("slab", "blk")),
        P("bag", ("slab", "blk")),
        P(("slab", "blk", "sub"), None),
        P(("slab", "blk", "sub"), None),
        P(("slab", "blk", "sub")),
    )
    return jax.shard_map(
        make_shards(mesh.shape["blk"], mesh.shape["sub"]),
        mesh=mesh,
        in_specs=placed,
        out_specs=(P("bag", ("slab", "blk")), P("bag", ("slab", "blk"))),
        check_vma=False,
    )
```
